768 devices in a mesh: seq: 96 (over z, x, core), head: 8 (over y).
Axes of the slice: x: 4, y: 8, z: 12, core: 2. Of those that a mesh axis runs over, the one named last changes fastest.
Arguments:
- query_rows: bfloat16 [12288, 8192], P('seq', 'head'), may hold values from -6 to 6
- key_rows: bfloat16 [12288, 8192], P('seq', 'head'), may hold values from -6 to 6
- value_rows: bfloat16 [12288, 8192], P('seq', 'head'), may hold values from -24 to 24
- grad_rows: bfloat16 [12288, 8192], P('seq', 'head'), may hold values from -6 to 6
- norm_gain: bfloat16 [8192], P('head'), may hold values from 0.5 to 1.5
- doc_start: int32 [12288], P('seq'), may hold values from 0 to 12287, as said below
Outputs:
- normed: bfloat16 [12288, 8192], P('seq', 'head')
- grad_query: bfloat16 [12288, 8192], P('seq', 'head')
- grad_key: bfloat16 [12288, 8192], P('seq', 'head')
- grad_value: bfloat16 [12288, 8192], P('seq', 'head')
The draws below stay inside these ranges and needn't reach their ends.
Inputs may be any that keep to these rules, and one draw needn't show every extreme that they name: doc_start[0] = 0; doc_start never falls, doc_start[t] <= t, and doc_start[t] == t exactly where a document begins. The document that holds token 0 ends after token 6144 and before token 9216. The last token begins a document of its own.
All inputs are finite; a program needn't handle non-finite values.
Results may differ from the reference program's by a relative error of at most 0.0058.
Values sent between devices are 32-bit elements; how exact they have to be, the bound alone decides.
No kernel may reach another device: no remote copies, remote signals or barrier semaphores. Data moves between devices by JAX's collectives and lax.ppermute only.
A program may use at most 128 MiB of HBM per device.

```python
import jax
import jax.numpy as jnp
from jax import lax

HEADS = 64
DH = 128
TOK_DEV = 128
TOKENS = 12288
WIDTH = 8192


def draw_doc_start(key, part):
    blocks = TOKENS // TOK_DEV
    key_end, key_offset, key_cut, key_pick = jax.random.split(key, 4)
    end_block = jax.random.randint(key_end, (), blocks // 2, 3 * blocks // 4)
    end_token = end_block * TOK_DEV + jax.random.randint(key_offset, (), 1, TOK_DEV)
    block_ids = jnp.arange(blocks, dtype=jnp.int32)
    drawn_block = end_block + 1
    split_block = (end_block + 1 + blocks) // 2
    cut_blocks = jax.random.randint(key_cut, (blocks,), 0, 2)
    cut_blocks = jnp.where(block_ids == drawn_block, 0, cut_blocks)
    cut_blocks = jnp.where(block_ids == split_block, 1, cut_blocks)
    picked = jax.random.randint(key_pick, (TOKENS,), 0, TOK_DEV) < 3
    positions = jnp.arange(TOKENS, dtype=jnp.int32)
    block_of = positions // TOK_DEV
    begins = (cut_blocks[block_of] == 1) & picked & (positions > end_token)
    begins = begins | (positions == end_token) | (positions == 0) | (positions == TOKENS - 1)
    begins = begins | (positions == drawn_block * TOK_DEV) | (positions == split_block * TOK_DEV)
    marks = jnp.where(begins, positions, 0).astype(jnp.int32)
    return lax.cummax(marks, axis=0)


def draw_value_rows(key, part):
    key_base, key_jitter = jax.random.split(key, 2)
    level = jnp.arange(HEADS, dtype=jnp.float32) / max(HEADS - 1, 1)
    base = jnp.clip(jax.random.normal(key_base, (TOKENS, HEADS, DH), jnp.float32), -5.0, 5.0)
    rise = jnp.power(10.0, level) / 3.0
    jitter = jnp.power(2.0, jax.random.uniform(key_jitter, (HEADS,), jnp.float32, -0.5, 0.5))
    return (base * (rise * jitter)[None, :, None]).reshape(TOKENS, HEADS * DH).astype(jnp.bfloat16)


def level_of(own_key, shape, pieces, low, top_value):
    factor_of, own = 1.0, jax.random.fold_in(own_key, 6)
    for dim, blocks in pieces:
        heights = jnp.exp(jax.random.uniform(jax.random.fold_in(own, dim), (blocks,), jnp.float32, low / len(pieces), top_value / len(pieces)))
        factor_of = factor_of * jnp.repeat(heights, shape[dim] // blocks).reshape([-1 if axis == dim else 1 for axis in range(len(shape))])
    return factor_of


def bell_draw(rng, extent, width, bound, pieces=(), kind=jnp.bfloat16):
    level = level_of(rng, extent, pieces, -0.22, 0.18) if pieces else 1.0
    array = jax.random.normal(rng, extent, jnp.float32) * width * level
    return jnp.minimum(jnp.maximum(array, -bound), bound).astype(kind)


def setup_inputs(seed: int = 0) -> dict:
    key_of = jax.random.split(jax.random.key(seed), 7)
    return {
        "query_rows": bell_draw(key_of[0], (TOKENS, WIDTH), 1.0, 6.0, ((0, 96), (1, 8))),
        "key_rows": bell_draw(key_of[1], (TOKENS, WIDTH), 1.0, 6.0, ((0, 96), (1, 8))),
        "value_rows": draw_value_rows(jax.random.fold_in(key_of[6], 71), 0),
        "grad_rows": bell_draw(key_of[3], (TOKENS, WIDTH), 1.0, 6.0, ((0, 96), (1, 8))),
        "norm_gain": jnp.clip(1.0 + 0.1 * jax.random.normal(key_of[4], (WIDTH,), jnp.float32), 0.5, 1.5).astype(jnp.bfloat16),
        "doc_start": draw_doc_start(jax.random.fold_in(key_of[6], 71), 0),
    }


def same_document(starts_blk):
    index_vec = jnp.arange(starts_blk.shape[0], dtype=jnp.int32)
    return (starts_blk[:, None] == starts_blk[None, :]) & (index_vec[None, :] <= index_vec[:, None])

def masked_scores(left_rows, right_rows, causal):
    scores = jnp.einsum('thd,shd->hts', left_rows.astype(jnp.float32), right_rows.astype(jnp.float32))
    return jnp.where(causal[None], scores, 0.0).astype(jnp.bfloat16)

def reference(query_rows, key_rows, value_rows, grad_rows, norm_gain, doc_start):
    blocks = TOKENS // TOK_DEV
    block_shape = (blocks, TOK_DEV, HEADS, DH)
    queries = query_rows.reshape(block_shape)
    key_vecs = key_rows.reshape(block_shape)
    value_vecs = value_rows.reshape(block_shape)
    grad_vecs = grad_rows.reshape(block_shape)
    starts = doc_start.reshape(blocks, TOK_DEV)
    gain_rows = norm_gain.astype(jnp.float32).reshape(HEADS, DH)
    anchors = jnp.arange(blocks, dtype=jnp.int32) * TOK_DEV

    def forward_step(state_in, inputs):
        queries_blk, keys_blk, values_blk, grads_blk, starts_blk, anchor = inputs
        causal = same_document(starts_blk)
        prefix = jnp.where(starts_blk[0] < anchor, state_in, 0.0)
        prefix_low = prefix.astype(jnp.bfloat16)
        mask_first = (starts_blk < anchor).astype(jnp.float32)[:, None, None]
        weights = masked_scores(queries_blk, keys_blk, causal)
        outputs = jnp.einsum('hts,she->the', weights.astype(jnp.float32), values_blk.astype(jnp.float32))
        outputs = outputs + mask_first * jnp.einsum('thd,hde->the', queries_blk.astype(jnp.float32), prefix_low.astype(jnp.float32))
        sum_squares = lax.optimization_barrier(jnp.sum(outputs * outputs, axis=(1, 2)))
        inv_rms = lax.rsqrt(sum_squares / WIDTH + 1e-06)
        normed = (outputs * inv_rms[:, None, None] * gain_rows).astype(jnp.bfloat16)
        scaled = grads_blk.astype(jnp.float32) * gain_rows
        inner = lax.optimization_barrier(jnp.sum(scaled * outputs, axis=(1, 2)))
        grad_out = (inv_rms[:, None, None] * (scaled - outputs * (inner * inv_rms * inv_rms / WIDTH)[:, None, None])).astype(jnp.bfloat16)
        back_weights = masked_scores(grad_out, values_blk, causal)
        grad_query = jnp.einsum('hts,shd->thd', back_weights.astype(jnp.float32), keys_blk.astype(jnp.float32))
        grad_query = grad_query + mask_first * jnp.einsum('the,hde->thd', grad_out.astype(jnp.float32), prefix_low.astype(jnp.float32))
        mask_last = (starts_blk == starts_blk[-1]).astype(jnp.bfloat16)[:, None, None]
        local_state = jnp.einsum('thd,the->hde', (keys_blk * mask_last).astype(jnp.float32), values_blk.astype(jnp.float32))
        state_out = local_state + jnp.where(starts_blk[-1] < anchor, prefix, 0.0)
        return (state_out, (normed, grad_out, grad_query.astype(jnp.bfloat16)))
    state_zero = jnp.zeros((HEADS, DH, DH), jnp.float32)
    final_state, (normed, grad_outs, grad_query) = lax.scan(forward_step, state_zero, (queries, key_vecs, value_vecs, grad_vecs, starts, anchors))
    next_first = jnp.concatenate([starts[1:, 0], jnp.full((1,), TOKENS, dtype=jnp.int32)])
    continues = next_first < anchors + TOK_DEV

    def backward_step(state_in, inputs):
        queries_blk, keys_blk, values_blk, grad_out, starts_blk, continue_flag = inputs
        causal = same_document(starts_blk)
        suffix = jnp.where(continue_flag, state_in, 0.0)
        suffix_low = suffix.astype(jnp.bfloat16).astype(jnp.float32)
        weights = masked_scores(queries_blk, keys_blk, causal)
        back_weights = masked_scores(grad_out, values_blk, causal)
        mask_last = (starts_blk == starts_blk[-1]).astype(jnp.float32)[:, None, None]
        grad_key = jnp.einsum('hts,thd->shd', back_weights.astype(jnp.float32), queries_blk.astype(jnp.float32))
        grad_key = grad_key + mask_last * jnp.einsum('she,hde->shd', values_blk.astype(jnp.float32), suffix_low)
        grad_value = jnp.einsum('hts,the->she', weights.astype(jnp.float32), grad_out.astype(jnp.float32))
        grad_value = grad_value + mask_last * jnp.einsum('shd,hde->she', keys_blk.astype(jnp.float32), suffix_low)
        mask_head = (starts_blk == starts_blk[0]).astype(jnp.bfloat16)[:, None, None]
        local_state = jnp.einsum('thd,the->hde', (queries_blk * mask_head).astype(jnp.float32), grad_out.astype(jnp.float32))
        state_out = local_state + jnp.where(starts_blk[-1] == starts_blk[0], suffix, 0.0)
        return (state_out, (grad_key.astype(jnp.bfloat16), grad_value.astype(jnp.bfloat16)))
    first_state, (grad_key, grad_value) = lax.scan(backward_step, state_zero, (queries, key_vecs, value_vecs, grad_outs, starts, continues), reverse=True)
    flat = (TOKENS, WIDTH)
    return (normed.reshape(flat), grad_query.reshape(flat), grad_key.reshape(flat), grad_value.reshape(flat))
```

```python
import jax
import jax.numpy as jnp
from jax import lax
from jax.sharding import Mesh
from jax.sharding import PartitionSpec as P

DH = 128
WIDTH = 8192
SEQ = ("zs", "slab")


def causal_scores(left_rows, right_rows, causal):
    scores = jnp.einsum("thd,shd->hts", left_rows, right_rows, preferred_element_type=jnp.float32)
    return jnp.where(causal[None], scores, 0.0).astype(jnp.bfloat16)


def weighted_sum(weights, pieces):
    return jnp.sum(weights[:, :, None, None] * pieces[None], axis=1)


def head_table(head_start, tokens_here):
    in_slab = lax.all_gather(head_start, "slab")
    table = lax.all_gather(in_slab, "zs")
    return table.reshape(-1) // tokens_here


def forward_prefix(local_state, first_block):
    slabs = lax.axis_size("zs")
    group = lax.axis_size("slab")
    slab_index = lax.axis_index("zs")
    slab_first = slab_index * group
    blocks = slab_first + jnp.arange(group, dtype=jnp.int32)
    pieces = lax.all_to_all(local_state, "slab", 0, 0, tiled=True)
    lows = first_block[blocks]
    inner = (blocks[None, :] < blocks[:, None]) & (blocks[None, :] >= lows[:, None])
    in_slab = weighted_sum(inner.astype(jnp.float32), pieces)
    next_low = first_block[jnp.minimum(slab_first + group, slabs * group - 1)]
    keep = (blocks >= next_low) & (slab_index + 1 < slabs)
    aggregate = jnp.sum(keep.astype(jnp.float32)[:, None, None] * pieces, axis=0)
    gathered = lax.all_gather(aggregate, "zs")
    slab_ids = jnp.arange(slabs, dtype=jnp.int32)
    low_slab = first_block[slab_first] // group
    take = (slab_ids < slab_index) & (slab_ids >= low_slab)
    earlier = jnp.sum(take.astype(jnp.float32)[:, None, None] * gathered, axis=0)
    reaches = (lows < slab_first).astype(jnp.float32)[:, None, None]
    prefix = in_slab + reaches * earlier[None]
    return lax.all_to_all(prefix, "slab", 0, 0, tiled=True)


def backward_suffix(local_state, first_block):
    slabs = lax.axis_size("zs")
    group = lax.axis_size("slab")
    slab_index = lax.axis_index("zs")
    slab_first = slab_index * group
    blocks = slab_first + jnp.arange(group, dtype=jnp.int32)
    pieces = lax.all_to_all(local_state, "slab", 0, 0, tiled=True)
    lows = first_block[blocks]
    inner = (blocks[None, :] > blocks[:, None]) & (lows[None, :] <= blocks[:, None])
    in_slab = weighted_sum(inner.astype(jnp.float32), pieces)
    keep = lows < slab_first
    aggregate = jnp.sum(keep.astype(jnp.float32)[:, None, None] * pieces, axis=0)
    gathered = lax.all_gather(aggregate, "zs")
    slab_ids = jnp.arange(slabs, dtype=jnp.int32)
    slab_lows = first_block[slab_ids * group]
    take = (slab_ids[None, :] > slab_index) & (slab_lows[None, :] <= blocks[:, None])
    later = weighted_sum(take.astype(jnp.float32), gathered)
    suffix = in_slab + later
    return lax.all_to_all(suffix, "slab", 0, 0, tiled=True)


def on_device(query_rows, key_rows, value_rows, grad_rows, norm_gain, doc_start):
    tokens_here = query_rows.shape[0]
    heads_here = query_rows.shape[1] // DH
    block_shape = (tokens_here, heads_here, DH)
    queries = query_rows.reshape(block_shape)
    key_vecs = key_rows.reshape(block_shape)
    value_vecs = value_rows.reshape(block_shape)
    grad_vecs = grad_rows.reshape(block_shape)
    gain_rows = norm_gain.astype(jnp.float32).reshape(heads_here, DH)
    block = lax.axis_index("zs") * lax.axis_size("slab") + lax.axis_index("slab")
    anchor = block * tokens_here
    positions = jnp.arange(tokens_here, dtype=jnp.int32)
    causal = (doc_start[:, None] == doc_start[None, :]) & (positions[None, :] <= positions[:, None])
    last_start = doc_start[-1]
    head_start = doc_start[0]
    first_block = head_table(head_start, tokens_here)
    mask_last = (doc_start == last_start).astype(jnp.bfloat16)[:, None, None]
    local_state = jnp.einsum(
        "thd,the->hde", key_vecs * mask_last, value_vecs, preferred_element_type=jnp.float32
    )
    opens_before = (head_start < anchor).astype(jnp.float32)
    prefix_low = (forward_prefix(local_state, first_block) * opens_before).astype(jnp.bfloat16)
    mask_first = (doc_start < anchor).astype(jnp.float32)[:, None, None]
    weights = causal_scores(queries, key_vecs, causal)
    outputs = jnp.einsum("hts,she->the", weights, value_vecs, preferred_element_type=jnp.float32)
    outputs = outputs + mask_first * jnp.einsum(
        "thd,hde->the", queries, prefix_low, preferred_element_type=jnp.float32
    )
    scaled = grad_vecs.astype(jnp.float32) * gain_rows
    totals = lax.psum(
        (jnp.sum(outputs * outputs, axis=(1, 2)), jnp.sum(scaled * outputs, axis=(1, 2))), "head"
    )
    inv_rms = lax.rsqrt(totals[0] / WIDTH + 1e-06)
    normed = (outputs * inv_rms[:, None, None] * gain_rows).astype(jnp.bfloat16)
    grad_out = (
        inv_rms[:, None, None]
        * (scaled - outputs * (totals[1] * inv_rms * inv_rms / WIDTH)[:, None, None])
    ).astype(jnp.bfloat16)
    back_weights = causal_scores(grad_out, value_vecs, causal)
    grad_query = jnp.einsum(
        "hts,shd->thd", back_weights, key_vecs, preferred_element_type=jnp.float32
    )
    grad_query = grad_query + mask_first * jnp.einsum(
        "the,hde->thd", grad_out, prefix_low, preferred_element_type=jnp.float32
    )
    mask_head = (doc_start == head_start).astype(jnp.bfloat16)[:, None, None]
    back_state = jnp.einsum(
        "thd,the->hde", queries * mask_head, grad_out, preferred_element_type=jnp.float32
    )
    next_block = jnp.minimum(block + 1, first_block.shape[0] - 1)
    continues = (block + 1 < first_block.shape[0]) & (first_block[next_block] <= block)
    suffix = backward_suffix(back_state, first_block) * continues.astype(jnp.float32)
    suffix_low = suffix.astype(jnp.bfloat16)
    mask_tail = mask_last.astype(jnp.float32)
    grad_key = jnp.einsum("hts,thd->shd", back_weights, queries, preferred_element_type=jnp.float32)
    grad_key = grad_key + mask_tail * jnp.einsum(
        "she,hde->shd", value_vecs, suffix_low, preferred_element_type=jnp.float32
    )
    grad_value = jnp.einsum("hts,the->she", weights, grad_out, preferred_element_type=jnp.float32)
    grad_value = grad_value + mask_tail * jnp.einsum(
        "shd,hde->she", key_vecs, suffix_low, preferred_element_type=jnp.float32
    )
    flat = (tokens_here, heads_here * DH)
    return (
        normed.reshape(flat),
        grad_query.astype(jnp.bfloat16).reshape(flat),
        grad_key.astype(jnp.bfloat16).reshape(flat),
        grad_value.astype(jnp.bfloat16).reshape(flat),
    )


def solution(mesh):
    seq_count = mesh.shape["seq"]
    group = WIDTH // DH // mesh.shape["head"]
    slabbed = Mesh(
        mesh.devices.reshape(seq_count // group, group, mesh.shape["head"]), ("zs", "slab", "head")
    )
    rows = P(SEQ, "head")
    placed = (rows, rows, rows, rows, P("head"), P(SEQ))
    return jax.shard_map(
        on_device,
        mesh=slabbed,
        in_specs=placed,
        out_specs=(rows, rows, rows, rows),
        check_vma=False,
    )
```

```python
import jax
import jax.numpy as jnp
from jax import lax
from jax.sharding import Mesh
from jax.sharding import PartitionSpec as P

DH = 128
WIDTH = 8192
SEQ = ("zs", "slab")


def causal_scores(left_rows, right_rows, causal):
    scores = jnp.einsum("thd,shd->hts", left_rows, right_rows, preferred_element_type=jnp.float32)
    return jnp.where(causal[None], scores, 0.0).astype(jnp.bfloat16)


def weighted_sum(weights, pieces):
    return jnp.sum(weights[:, :, None, None] * pieces[None], axis=1)


def with_rows(state, values):
    rows = jnp.zeros((state.shape[0], 8, state.shape[2]), jnp.float32)
    rows = rows.at[:, : values.shape[0], :].set(values.astype(jnp.float32)[None, :, None])
    return jnp.concatenate([state, rows], axis=1)


def forward_prefix(local_state, head_start, last_start, tokens_here):
    slabs = lax.axis_size("zs")
    group = lax.axis_size("slab")
    slab_index = lax.axis_index("zs")
    slab_first = slab_index * group
    blocks = slab_first + jnp.arange(group, dtype=jnp.int32)
    width = local_state.shape[1]
    payload = with_rows(local_state, jnp.stack([head_start, last_start]))
    arrived = lax.all_to_all(payload, "slab", 0, 0, tiled=True)
    pieces = arrived[:, :width]
    lows = arrived[:, width, 0].astype(jnp.int32) // tokens_here
    tail_low = arrived[group - 1, width + 1, 0].astype(jnp.int32) // tokens_here
    inner = (blocks[None, :] < blocks[:, None]) & (blocks[None, :] >= lows[:, None])
    in_slab = weighted_sum(inner.astype(jnp.float32), pieces)
    keep = blocks >= tail_low
    aggregate = jnp.sum(keep.astype(jnp.float32)[:, None, None] * pieces, axis=0)
    sent = with_rows(aggregate[None], arrived[0, width, 0:1])[0]
    gathered = lax.all_gather(sent, "zs")
    slab_lows = gathered[:, width, 0].astype(jnp.int32) // tokens_here
    slab_ids = jnp.arange(slabs, dtype=jnp.int32)
    take = (slab_ids < slab_index) & (slab_ids >= lows[0] // group)
    earlier = jnp.sum(take.astype(jnp.float32)[:, None, None] * gathered[:, :width], axis=0)
    reaches = (lows < slab_first).astype(jnp.float32)[:, None, None]
    prefix = in_slab + reaches * earlier[None]
    return lax.all_to_all(prefix, "slab", 0, 0, tiled=True), lows, slab_lows


def backward_suffix(local_state, lows, slab_lows):
    slabs = lax.axis_size("zs")
    group = lax.axis_size("slab")
    slab_index = lax.axis_index("zs")
    slab_first = slab_index * group
    blocks = slab_first + jnp.arange(group, dtype=jnp.int32)
    pieces = lax.all_to_all(local_state, "slab", 0, 0, tiled=True)
    inner = (blocks[None, :] > blocks[:, None]) & (lows[None, :] <= blocks[:, None])
    in_slab = weighted_sum(inner.astype(jnp.float32), pieces)
    keep = lows < slab_first
    aggregate = jnp.sum(keep.astype(jnp.float32)[:, None, None] * pieces, axis=0)
    gathered = lax.all_gather(aggregate, "zs")
    slab_ids = jnp.arange(slabs, dtype=jnp.int32)
    take = (slab_ids[None, :] > slab_index) & (slab_lows[None, :] <= blocks[:, None])
    later = weighted_sum(take.astype(jnp.float32), gathered)
    suffix = in_slab + later
    return lax.all_to_all(suffix, "slab", 0, 0, tiled=True)


def on_device(query_rows, key_rows, value_rows, grad_rows, norm_gain, doc_start):
    tokens_here = query_rows.shape[0]
    heads_here = query_rows.shape[1] // DH
    block_shape = (tokens_here, heads_here, DH)
    queries = query_rows.reshape(block_shape)
    key_vecs = key_rows.reshape(block_shape)
    value_vecs = value_rows.reshape(block_shape)
    grad_vecs = grad_rows.reshape(block_shape)
    gain_rows = norm_gain.astype(jnp.float32).reshape(heads_here, DH)
    block = lax.axis_index("zs") * lax.axis_size("slab") + lax.axis_index("slab")
    anchor = block * tokens_here
    positions = jnp.arange(tokens_here, dtype=jnp.int32)
    causal = (doc_start[:, None] == doc_start[None, :]) & (positions[None, :] <= positions[:, None])
    last_start = doc_start[-1]
    head_start = doc_start[0]
    mask_last = (doc_start == last_start).astype(jnp.bfloat16)[:, None, None]
    local_state = jnp.einsum(
        "thd,the->hde", key_vecs * mask_last, value_vecs, preferred_element_type=jnp.float32
    )
    opens_before = (head_start < anchor).astype(jnp.float32)
    prefix, lows, slab_lows = forward_prefix(local_state, head_start, last_start, tokens_here)
    prefix_low = (prefix * opens_before).astype(jnp.bfloat16)
    mask_first = (doc_start < anchor).astype(jnp.float32)[:, None, None]
    weights = causal_scores(queries, key_vecs, causal)
    outputs = jnp.einsum("hts,she->the", weights, value_vecs, preferred_element_type=jnp.float32)
    outputs = outputs + mask_first * jnp.einsum(
        "thd,hde->the", queries, prefix_low, preferred_element_type=jnp.float32
    )
    scaled = grad_vecs.astype(jnp.float32) * gain_rows
    totals = lax.psum(
        (jnp.sum(outputs * outputs, axis=(1, 2)), jnp.sum(scaled * outputs, axis=(1, 2))), "head"
    )
    inv_rms = lax.rsqrt(totals[0] / WIDTH + 1e-06)
    normed = (outputs * inv_rms[:, None, None] * gain_rows).astype(jnp.bfloat16)
    grad_out = (
        inv_rms[:, None, None]
        * (scaled - outputs * (totals[1] * inv_rms * inv_rms / WIDTH)[:, None, None])
    ).astype(jnp.bfloat16)
    back_weights = causal_scores(grad_out, value_vecs, causal)
    grad_query = jnp.einsum(
        "hts,shd->thd", back_weights, key_vecs, preferred_element_type=jnp.float32
    )
    grad_query = grad_query + mask_first * jnp.einsum(
        "the,hde->thd", grad_out, prefix_low, preferred_element_type=jnp.float32
    )
    mask_head = (doc_start == head_start).astype(jnp.bfloat16)[:, None, None]
    back_state = jnp.einsum(
        "thd,the->hde", queries * mask_head, grad_out, preferred_element_type=jnp.float32
    )
    slab_place = lax.axis_index("slab")
    slab_next = jnp.minimum(lax.axis_index("zs") + 1, slab_lows.shape[0] - 1)
    next_low = jnp.where(
        slab_place + 1 < lows.shape[0],
        lows[jnp.minimum(slab_place + 1, lows.shape[0] - 1)],
        slab_lows[slab_next],
    )
    continues = (block + 1 < lows.shape[0] * slab_lows.shape[0]) & (next_low <= block)
    suffix = backward_suffix(back_state, lows, slab_lows) * continues.astype(jnp.float32)
    suffix_low = suffix.astype(jnp.bfloat16)
    mask_tail = mask_last.astype(jnp.float32)
    grad_key = jnp.einsum("hts,thd->shd", back_weights, queries, preferred_element_type=jnp.float32)
    grad_key = grad_key + mask_tail * jnp.einsum(
        "she,hde->shd", value_vecs, suffix_low, preferred_element_type=jnp.float32
    )
    grad_value = jnp.einsum("hts,the->she", weights, grad_out, preferred_element_type=jnp.float32)
    grad_value = grad_value + mask_tail * jnp.einsum(
        "shd,hde->she", key_vecs, suffix_low, preferred_element_type=jnp.float32
    )
    flat = (tokens_here, heads_here * DH)
    return (
        normed.reshape(flat),
        grad_query.astype(jnp.bfloat16).reshape(flat),
        grad_key.astype(jnp.bfloat16).reshape(flat),
        grad_value.astype(jnp.bfloat16).reshape(flat),
    )


def solution(mesh):
    seq_count = mesh.shape["seq"]
    group = WIDTH // DH // mesh.shape["head"]
    slabbed = Mesh(
        mesh.devices.reshape(seq_count // group, group, mesh.shape["head"]), ("zs", "slab", "head")
    )
    rows = P(SEQ, "head")
    placed = (rows, rows, rows, rows, P("head"), P(SEQ))
    return jax.shard_map(
        on_device,
        mesh=slabbed,
        in_specs=placed,
        out_specs=(rows, rows, rows, rows),
        check_vma=False,
    )
```

```python
import jax
import jax.numpy as jnp
from jax import lax
from jax.sharding import Mesh
from jax.sharding import PartitionSpec as P

DH = 128
WIDTH = 8192
SEQ = ("zs", "slab")
SLAB = 16


def causal_scores(left_rows, right_rows, causal):
    scores = jnp.einsum("thd,shd->hts", left_rows, right_rows, preferred_element_type=jnp.float32)
    return jnp.where(causal[None], scores, 0.0).astype(jnp.bfloat16)


def weighted_sum(weights, pieces):
    return jnp.sum(weights[:, :, None, None] * pieces[None], axis=1)


def with_rows(state, values):
    rows = jnp.zeros((state.shape[0], 8, state.shape[2]), jnp.float32)
    rows = rows.at[:, : values.shape[0], :].set(values.astype(jnp.float32)[None, :, None])
    return jnp.concatenate([state, rows], axis=1)


def forward_prefix(local_state, head_start, last_start, tokens_here):
    slabs = lax.axis_size("zs")
    group = lax.axis_size("slab")
    slab_index = lax.axis_index("zs")
    slab_first = slab_index * group
    blocks = slab_first + jnp.arange(group, dtype=jnp.int32)
    heads, rows, lanes = local_state.shape
    width = heads * rows // group
    payload = with_rows(local_state.reshape(group, width, lanes), jnp.stack([head_start, last_start]))
    arrived = lax.all_to_all(payload, "slab", 0, 0, tiled=True)
    pieces = arrived[:, :width]
    lows = arrived[:, width, 0].astype(jnp.int32) // tokens_here
    tail_low = arrived[group - 1, width + 1, 0].astype(jnp.int32) // tokens_here
    inner = (blocks[None, :] < blocks[:, None]) & (blocks[None, :] >= lows[:, None])
    in_slab = weighted_sum(inner.astype(jnp.float32), pieces)
    keep = blocks >= tail_low
    aggregate = jnp.sum(keep.astype(jnp.float32)[:, None, None] * pieces, axis=0)
    sent = with_rows(aggregate[None], arrived[0, width, 0:1])[0]
    gathered = lax.all_gather(sent, "zs")
    slab_lows = gathered[:, width, 0].astype(jnp.int32) // tokens_here
    slab_ids = jnp.arange(slabs, dtype=jnp.int32)
    take = (slab_ids < slab_index) & (slab_ids >= lows[0] // group)
    earlier = jnp.sum(take.astype(jnp.float32)[:, None, None] * gathered[:, :width], axis=0)
    reaches = (lows < slab_first).astype(jnp.float32)[:, None, None]
    prefix = in_slab + reaches * earlier[None]
    prefix = lax.all_to_all(prefix, "slab", 0, 0, tiled=True).reshape(heads, rows, lanes)
    return prefix, lows, slab_lows


def backward_suffix(local_state, lows, slab_lows):
    slabs = lax.axis_size("zs")
    group = lax.axis_size("slab")
    slab_index = lax.axis_index("zs")
    slab_first = slab_index * group
    blocks = slab_first + jnp.arange(group, dtype=jnp.int32)
    heads, rows, lanes = local_state.shape
    pieces = local_state.reshape(group, heads * rows // group, lanes)
    pieces = lax.all_to_all(pieces, "slab", 0, 0, tiled=True)
    inner = (blocks[None, :] > blocks[:, None]) & (lows[None, :] <= blocks[:, None])
    in_slab = weighted_sum(inner.astype(jnp.float32), pieces)
    keep = lows < slab_first
    aggregate = jnp.sum(keep.astype(jnp.float32)[:, None, None] * pieces, axis=0)
    gathered = lax.all_gather(aggregate, "zs")
    slab_ids = jnp.arange(slabs, dtype=jnp.int32)
    take = (slab_ids[None, :] > slab_index) & (slab_lows[None, :] <= blocks[:, None])
    later = weighted_sum(take.astype(jnp.float32), gathered)
    suffix = in_slab + later
    return lax.all_to_all(suffix, "slab", 0, 0, tiled=True).reshape(heads, rows, lanes)


def on_device(query_rows, key_rows, value_rows, grad_rows, norm_gain, doc_start):
    tokens_here = query_rows.shape[0]
    heads_here = query_rows.shape[1] // DH
    block_shape = (tokens_here, heads_here, DH)
    queries = query_rows.reshape(block_shape)
    key_vecs = key_rows.reshape(block_shape)
    value_vecs = value_rows.reshape(block_shape)
    grad_vecs = grad_rows.reshape(block_shape)
    gain_rows = norm_gain.astype(jnp.float32).reshape(heads_here, DH)
    block = lax.axis_index("zs") * lax.axis_size("slab") + lax.axis_index("slab")
    anchor = block * tokens_here
    positions = jnp.arange(tokens_here, dtype=jnp.int32)
    causal = (doc_start[:, None] == doc_start[None, :]) & (positions[None, :] <= positions[:, None])
    last_start = doc_start[-1]
    head_start = doc_start[0]
    mask_last = (doc_start == last_start).astype(jnp.bfloat16)[:, None, None]
    local_state = jnp.einsum(
        "thd,the->hde", key_vecs * mask_last, value_vecs, preferred_element_type=jnp.float32
    )
    opens_before = (head_start < anchor).astype(jnp.float32)
    prefix, lows, slab_lows = forward_prefix(local_state, head_start, last_start, tokens_here)
    prefix_low = (prefix * opens_before).astype(jnp.bfloat16)
    mask_first = (doc_start < anchor).astype(jnp.float32)[:, None, None]
    weights = causal_scores(queries, key_vecs, causal)
    outputs = jnp.einsum("hts,she->the", weights, value_vecs, preferred_element_type=jnp.float32)
    outputs = outputs + mask_first * jnp.einsum(
        "thd,hde->the", queries, prefix_low, preferred_element_type=jnp.float32
    )
    scaled = grad_vecs.astype(jnp.float32) * gain_rows
    totals = lax.psum(
        (jnp.sum(outputs * outputs, axis=(1, 2)), jnp.sum(scaled * outputs, axis=(1, 2))), "head"
    )
    inv_rms = lax.rsqrt(totals[0] / WIDTH + 1e-06)
    normed = (outputs * inv_rms[:, None, None] * gain_rows).astype(jnp.bfloat16)
    grad_out = (
        inv_rms[:, None, None]
        * (scaled - outputs * (totals[1] * inv_rms * inv_rms / WIDTH)[:, None, None])
    ).astype(jnp.bfloat16)
    back_weights = causal_scores(grad_out, value_vecs, causal)
    grad_query = jnp.einsum(
        "hts,shd->thd", back_weights, key_vecs, preferred_element_type=jnp.float32
    )
    grad_query = grad_query + mask_first * jnp.einsum(
        "the,hde->thd", grad_out, prefix_low, preferred_element_type=jnp.float32
    )
    mask_head = (doc_start == head_start).astype(jnp.bfloat16)[:, None, None]
    back_state = jnp.einsum(
        "thd,the->hde", queries * mask_head, grad_out, preferred_element_type=jnp.float32
    )
    slab_place = lax.axis_index("slab")
    slab_next = jnp.minimum(lax.axis_index("zs") + 1, slab_lows.shape[0] - 1)
    next_low = jnp.where(
        slab_place + 1 < lows.shape[0],
        lows[jnp.minimum(slab_place + 1, lows.shape[0] - 1)],
        slab_lows[slab_next],
    )
    continues = (block + 1 < lows.shape[0] * slab_lows.shape[0]) & (next_low <= block)
    suffix = backward_suffix(back_state, lows, slab_lows) * continues.astype(jnp.float32)
    suffix_low = suffix.astype(jnp.bfloat16)
    mask_tail = mask_last.astype(jnp.float32)
    grad_key = jnp.einsum("hts,thd->shd", back_weights, queries, preferred_element_type=jnp.float32)
    grad_key = grad_key + mask_tail * jnp.einsum(
        "she,hde->shd", value_vecs, suffix_low, preferred_element_type=jnp.float32
    )
    grad_value = jnp.einsum("hts,the->she", weights, grad_out, preferred_element_type=jnp.float32)
    grad_value = grad_value + mask_tail * jnp.einsum(
        "shd,hde->she", key_vecs, suffix_low, preferred_element_type=jnp.float32
    )
    flat = (tokens_here, heads_here * DH)
    return (
        normed.reshape(flat),
        grad_query.astype(jnp.bfloat16).reshape(flat),
        grad_key.astype(jnp.bfloat16).reshape(flat),
        grad_value.astype(jnp.bfloat16).reshape(flat),
    )


def solution(mesh):
    seq_count = mesh.shape["seq"]
    group = SLAB if seq_count % SLAB == 0 else 1
    slabbed = Mesh(
        mesh.devices.reshape(seq_count // group, group, mesh.shape["head"]), ("zs", "slab", "head")
    )
    rows = P(SEQ, "head")
    placed = (rows, rows, rows, rows, P("head"), P(SEQ))
    return jax.shard_map(
        on_device,
        mesh=slabbed,
        in_specs=placed,
        out_specs=(rows, rows, rows, rows),
        check_vma=False,
    )
```

```python
import jax
import jax.numpy as jnp
from jax import lax
from jax.sharding import Mesh
from jax.sharding import PartitionSpec as P

DH = 128
WIDTH = 8192
SEQ = ("zs", "slab")
SLAB = 16


def causal_scores(left_rows, right_rows, causal):
    scores = jnp.einsum("thd,shd->hts", left_rows, right_rows, preferred_element_type=jnp.float32)
    return jnp.where(causal[None], scores, 0.0).astype(jnp.bfloat16)


def weighted_sum(weights, pieces):
    return jnp.sum(weights[:, :, None, None] * pieces[None], axis=1)


def shifted(value, axis, by):
    peers = lax.axis_size(axis)
    pairs = [(i, i + by) for i in range(peers) if 0 <= i + by < peers]
    return lax.ppermute(value, axis, pairs)


def head_total(value):
    peers = lax.axis_size("head")
    bit = 1
    while bit < peers:
        value = value + lax.ppermute(value, "head", [(i, i ^ bit) for i in range(peers)])
        bit *= 2
    return value


def with_rows(state, values):
    rows = jnp.zeros((state.shape[0], 8, state.shape[2]), jnp.float32)
    rows = rows.at[:, : values.shape[0], :].set(values.astype(jnp.float32)[None, :, None])
    return jnp.concatenate([state, rows], axis=1)


def forward_prefix(local_state, head_start, last_start, tokens_here):
    slabs = lax.axis_size("zs")
    group = lax.axis_size("slab")
    slab_index = lax.axis_index("zs")
    slab_first = slab_index * group
    blocks = slab_first + jnp.arange(group, dtype=jnp.int32)
    heads, rows, lanes = local_state.shape
    width = heads * rows // group
    payload = with_rows(local_state.reshape(group, width, lanes), jnp.stack([head_start, last_start]))
    arrived = lax.all_to_all(payload, "slab", 0, 0, tiled=True)
    pieces = arrived[:, :width]
    lows = arrived[:, width, 0].astype(jnp.int32) // tokens_here
    tail_low = arrived[group - 1, width + 1, 0].astype(jnp.int32) // tokens_here
    inner = (blocks[None, :] < blocks[:, None]) & (blocks[None, :] >= lows[:, None])
    in_slab = weighted_sum(inner.astype(jnp.float32), pieces)
    keep = blocks >= tail_low
    aggregate = jnp.sum(keep.astype(jnp.float32)[:, None, None] * pieces, axis=0)
    earlier = jnp.zeros_like(aggregate)
    for offset in range(1, slabs):
        arrived_slab = shifted(aggregate, "zs", offset)
        take = (slab_index - offset >= lows[0] // group) & (slab_index >= offset)
        earlier = earlier + take.astype(jnp.float32) * arrived_slab
    reaches = (lows < slab_first).astype(jnp.float32)[:, None, None]
    prefix = in_slab + reaches * earlier[None]
    prefix = lax.all_to_all(prefix, "slab", 0, 0, tiled=True).reshape(heads, rows, lanes)
    return prefix, lows


def backward_suffix(local_state, lows):
    slabs = lax.axis_size("zs")
    group = lax.axis_size("slab")
    slab_index = lax.axis_index("zs")
    slab_first = slab_index * group
    blocks = slab_first + jnp.arange(group, dtype=jnp.int32)
    heads, rows, lanes = local_state.shape
    pieces = local_state.reshape(group, heads * rows // group, lanes)
    pieces = lax.all_to_all(pieces, "slab", 0, 0, tiled=True)
    inner = (blocks[None, :] > blocks[:, None]) & (lows[None, :] <= blocks[:, None])
    in_slab = weighted_sum(inner.astype(jnp.float32), pieces)
    keep = lows < slab_first
    aggregate = jnp.sum(keep.astype(jnp.float32)[:, None, None] * pieces, axis=0)
    width = aggregate.shape[0]
    sent = with_rows(aggregate[None], lows[0:1])[0]
    later = jnp.zeros_like(in_slab)
    for offset in range(1, slabs):
        arrived_slab = shifted(sent, "zs", -offset)
        slab_low = arrived_slab[width, 0].astype(jnp.int32)
        take = (slab_low <= blocks) & (slab_index + offset < slabs)
        later = later + take.astype(jnp.float32)[:, None, None] * arrived_slab[None, :width]
    suffix = in_slab + later
    return lax.all_to_all(suffix, "slab", 0, 0, tiled=True).reshape(heads, rows, lanes)


def on_device(query_rows, key_rows, value_rows, grad_rows, norm_gain, doc_start):
    tokens_here = query_rows.shape[0]
    heads_here = query_rows.shape[1] // DH
    block_shape = (tokens_here, heads_here, DH)
    queries = query_rows.reshape(block_shape)
    key_vecs = key_rows.reshape(block_shape)
    value_vecs = value_rows.reshape(block_shape)
    grad_vecs = grad_rows.reshape(block_shape)
    gain_rows = norm_gain.astype(jnp.float32).reshape(heads_here, DH)
    block = lax.axis_index("zs") * lax.axis_size("slab") + lax.axis_index("slab")
    anchor = block * tokens_here
    positions = jnp.arange(tokens_here, dtype=jnp.int32)
    causal = (doc_start[:, None] == doc_start[None, :]) & (positions[None, :] <= positions[:, None])
    last_start = doc_start[-1]
    head_start = doc_start[0]
    block_count = lax.axis_size(SEQ)
    next_head = shifted(head_start, SEQ, -1)
    mask_last = (doc_start == last_start).astype(jnp.bfloat16)[:, None, None]
    local_state = jnp.einsum(
        "thd,the->hde", key_vecs * mask_last, value_vecs, preferred_element_type=jnp.float32
    )
    opens_before = (head_start < anchor).astype(jnp.float32)
    prefix, lows = forward_prefix(local_state, head_start, last_start, tokens_here)
    prefix_low = (prefix * opens_before).astype(jnp.bfloat16)
    mask_first = (doc_start < anchor).astype(jnp.float32)[:, None, None]
    weights = causal_scores(queries, key_vecs, causal)
    outputs = jnp.einsum("hts,she->the", weights, value_vecs, preferred_element_type=jnp.float32)
    outputs = outputs + mask_first * jnp.einsum(
        "thd,hde->the", queries, prefix_low, preferred_element_type=jnp.float32
    )
    scaled = grad_vecs.astype(jnp.float32) * gain_rows
    totals = head_total(
        jnp.stack([jnp.sum(outputs * outputs, axis=(1, 2)), jnp.sum(scaled * outputs, axis=(1, 2))])
    )
    inv_rms = lax.rsqrt(totals[0] / WIDTH + 1e-06)
    normed = (outputs * inv_rms[:, None, None] * gain_rows).astype(jnp.bfloat16)
    grad_out = (
        inv_rms[:, None, None]
        * (scaled - outputs * (totals[1] * inv_rms * inv_rms / WIDTH)[:, None, None])
    ).astype(jnp.bfloat16)
    back_weights = causal_scores(grad_out, value_vecs, causal)
    grad_query = jnp.einsum(
        "hts,shd->thd", back_weights, key_vecs, preferred_element_type=jnp.float32
    )
    grad_query = grad_query + mask_first * jnp.einsum(
        "the,hde->thd", grad_out, prefix_low, preferred_element_type=jnp.float32
    )
    mask_head = (doc_start == head_start).astype(jnp.bfloat16)[:, None, None]
    back_state = jnp.einsum(
        "thd,the->hde", queries * mask_head, grad_out, preferred_element_type=jnp.float32
    )
    continues = (next_head // tokens_here <= block) & (block + 1 < block_count)
    suffix = backward_suffix(back_state, lows) * continues.astype(jnp.float32)
    suffix_low = suffix.astype(jnp.bfloat16)
    mask_tail = mask_last.astype(jnp.float32)
    grad_key = jnp.einsum("hts,thd->shd", back_weights, queries, preferred_element_type=jnp.float32)
    grad_key = grad_key + mask_tail * jnp.einsum(
        "she,hde->shd", value_vecs, suffix_low, preferred_element_type=jnp.float32
    )
    grad_value = jnp.einsum("hts,the->she", weights, grad_out, preferred_element_type=jnp.float32)
    grad_value = grad_value + mask_tail * jnp.einsum(
        "shd,hde->she", key_vecs, suffix_low, preferred_element_type=jnp.float32
    )
    flat = (tokens_here, heads_here * DH)
    return (
        normed.reshape(flat),
        grad_query.astype(jnp.bfloat16).reshape(flat),
        grad_key.astype(jnp.bfloat16).reshape(flat),
        grad_value.astype(jnp.bfloat16).reshape(flat),
    )


def solution(mesh):
    seq_count = mesh.shape["seq"]
    group = SLAB if seq_count % SLAB == 0 else 1
    slabbed = Mesh(
        mesh.devices.reshape(seq_count // group, group, mesh.shape["head"]), ("zs", "slab", "head")
    )
    rows = P(SEQ, "head")
    placed = (rows, rows, rows, rows, P("head"), P(SEQ))
    return jax.shard_map(
        on_device,
        mesh=slabbed,
        in_specs=placed,
        out_specs=(rows, rows, rows, rows),
        check_vma=False,
    )
```

```python
import jax
import jax.numpy as jnp
from jax import lax
from jax.sharding import Mesh
from jax.sharding import PartitionSpec as P

DH = 128
WIDTH = 8192
SEQ = ("zs", "slab")
SLAB = 32


def causal_scores(left_rows, right_rows, causal):
    scores = jnp.einsum("thd,shd->hts", left_rows, right_rows, preferred_element_type=jnp.float32)
    return jnp.where(causal[None], scores, 0.0).astype(jnp.bfloat16)


def weighted_sum(weights, pieces):
    return jnp.sum(weights[:, :, None, None] * pieces[None], axis=1)


def shifted(value, axis, by):
    peers = lax.axis_size(axis)
    pairs = [(i, i + by) for i in range(peers) if 0 <= i + by < peers]
    return lax.ppermute(value, axis, pairs)


def with_rows(state, values):
    rows = jnp.zeros((state.shape[0], 8, state.shape[2]), jnp.float32)
    rows = rows.at[:, : values.shape[0], :].set(values.astype(jnp.float32)[None, :, None])
    return jnp.concatenate([state, rows], axis=1)


def forward_prefix(local_state, head_start, last_start, tokens_here):
    slabs = lax.axis_size("zs")
    group = lax.axis_size("slab")
    slab_index = lax.axis_index("zs")
    slab_first = slab_index * group
    blocks = slab_first + jnp.arange(group, dtype=jnp.int32)
    heads, rows, lanes = local_state.shape
    width = heads * rows // group
    payload = with_rows(local_state.reshape(group, width, lanes), jnp.stack([head_start, last_start]))
    arrived = lax.all_to_all(payload, "slab", 0, 0, tiled=True)
    pieces = arrived[:, :width]
    lows = arrived[:, width, 0].astype(jnp.int32) // tokens_here
    tail_low = arrived[group - 1, width + 1, 0].astype(jnp.int32) // tokens_here
    inner = (blocks[None, :] < blocks[:, None]) & (blocks[None, :] >= lows[:, None])
    in_slab = weighted_sum(inner.astype(jnp.float32), pieces)
    keep = blocks >= tail_low
    aggregate = jnp.sum(keep.astype(jnp.float32)[:, None, None] * pieces, axis=0)
    earlier = jnp.zeros_like(aggregate)
    for offset in range(1, slabs):
        arrived_slab = shifted(aggregate, "zs", offset)
        take = (slab_index - offset >= lows[0] // group) & (slab_index >= offset)
        earlier = earlier + take.astype(jnp.float32) * arrived_slab
    reaches = (lows < slab_first).astype(jnp.float32)[:, None, None]
    prefix = in_slab + reaches * earlier[None]
    prefix = lax.all_to_all(prefix, "slab", 0, 0, tiled=True).reshape(heads, rows, lanes)
    return prefix, lows


def backward_suffix(local_state, lows):
    slabs = lax.axis_size("zs")
    group = lax.axis_size("slab")
    slab_index = lax.axis_index("zs")
    slab_first = slab_index * group
    blocks = slab_first + jnp.arange(group, dtype=jnp.int32)
    heads, rows, lanes = local_state.shape
    pieces = local_state.reshape(group, heads * rows // group, lanes)
    pieces = lax.all_to_all(pieces, "slab", 0, 0, tiled=True)
    inner = (blocks[None, :] > blocks[:, None]) & (lows[None, :] <= blocks[:, None])
    in_slab = weighted_sum(inner.astype(jnp.float32), pieces)
    keep = lows < slab_first
    aggregate = jnp.sum(keep.astype(jnp.float32)[:, None, None] * pieces, axis=0)
    width = aggregate.shape[0]
    sent = with_rows(aggregate[None], lows[0:1])[0]
    later = jnp.zeros_like(in_slab)
    for offset in range(1, slabs):
        arrived_slab = shifted(sent, "zs", -offset)
        slab_low = arrived_slab[width, 0].astype(jnp.int32)
        take = (slab_low <= blocks) & (slab_index + offset < slabs)
        later = later + take.astype(jnp.float32)[:, None, None] * arrived_slab[None, :width]
    suffix = in_slab + later
    return lax.all_to_all(suffix, "slab", 0, 0, tiled=True).reshape(heads, rows, lanes)


def on_device(query_rows, key_rows, value_rows, grad_rows, norm_gain, doc_start):
    tokens_here = query_rows.shape[0]
    heads_here = query_rows.shape[1] // DH
    block_shape = (tokens_here, heads_here, DH)
    queries = query_rows.reshape(block_shape)
    key_vecs = key_rows.reshape(block_shape)
    value_vecs = value_rows.reshape(block_shape)
    grad_vecs = grad_rows.reshape(block_shape)
    gain_rows = norm_gain.astype(jnp.float32).reshape(heads_here, DH)
    block = lax.axis_index("zs") * lax.axis_size("slab") + lax.axis_index("slab")
    anchor = block * tokens_here
    positions = jnp.arange(tokens_here, dtype=jnp.int32)
    causal = (doc_start[:, None] == doc_start[None, :]) & (positions[None, :] <= positions[:, None])
    last_start = doc_start[-1]
    head_start = doc_start[0]
    block_count = lax.axis_size(SEQ)
    next_head = shifted(head_start, SEQ, -1)
    mask_last = (doc_start == last_start).astype(jnp.bfloat16)[:, None, None]
    local_state = jnp.einsum(
        "thd,the->hde", key_vecs * mask_last, value_vecs, preferred_element_type=jnp.float32
    )
    opens_before = (head_start < anchor).astype(jnp.float32)
    prefix, lows = forward_prefix(local_state, head_start, last_start, tokens_here)
    prefix_low = (prefix * opens_before).astype(jnp.bfloat16)
    mask_first = (doc_start < anchor).astype(jnp.float32)[:, None, None]
    weights = causal_scores(queries, key_vecs, causal)
    outputs = jnp.einsum("hts,she->the", weights, value_vecs, preferred_element_type=jnp.float32)
    outputs = outputs + mask_first * jnp.einsum(
        "thd,hde->the", queries, prefix_low, preferred_element_type=jnp.float32
    )
    scaled = grad_vecs.astype(jnp.float32) * gain_rows
    totals = lax.psum(
        (jnp.sum(outputs * outputs, axis=(1, 2)), jnp.sum(scaled * outputs, axis=(1, 2))), "head"
    )
    inv_rms = lax.rsqrt(totals[0] / WIDTH + 1e-06)
    normed = (outputs * inv_rms[:, None, None] * gain_rows).astype(jnp.bfloat16)
    grad_out = (
        inv_rms[:, None, None]
        * (scaled - outputs * (totals[1] * inv_rms * inv_rms / WIDTH)[:, None, None])
    ).astype(jnp.bfloat16)
    back_weights = causal_scores(grad_out, value_vecs, causal)
    grad_query = jnp.einsum(
        "hts,shd->thd", back_weights, key_vecs, preferred_element_type=jnp.float32
    )
    grad_query = grad_query + mask_first * jnp.einsum(
        "the,hde->thd", grad_out, prefix_low, preferred_element_type=jnp.float32
    )
    mask_head = (doc_start == head_start).astype(jnp.bfloat16)[:, None, None]
    back_state = jnp.einsum(
        "thd,the->hde", queries * mask_head, grad_out, preferred_element_type=jnp.float32
    )
    continues = (next_head // tokens_here <= block) & (block + 1 < block_count)
    suffix = backward_suffix(back_state, lows) * continues.astype(jnp.float32)
    suffix_low = suffix.astype(jnp.bfloat16)
    mask_tail = mask_last.astype(jnp.float32)
    grad_key = jnp.einsum("hts,thd->shd", back_weights, queries, preferred_element_type=jnp.float32)
    grad_key = grad_key + mask_tail * jnp.einsum(
        "she,hde->shd", value_vecs, suffix_low, preferred_element_type=jnp.float32
    )
    grad_value = jnp.einsum("hts,the->she", weights, grad_out, preferred_element_type=jnp.float32)
    grad_value = grad_value + mask_tail * jnp.einsum(
        "shd,hde->she", key_vecs, suffix_low, preferred_element_type=jnp.float32
    )
    flat = (tokens_here, heads_here * DH)
    return (
        normed.reshape(flat),
        grad_query.astype(jnp.bfloat16).reshape(flat),
        grad_key.astype(jnp.bfloat16).reshape(flat),
        grad_value.astype(jnp.bfloat16).reshape(flat),
    )


def solution(mesh):
    seq_count = mesh.shape["seq"]
    group = SLAB if seq_count % SLAB == 0 else 1
    slabbed = Mesh(
        mesh.devices.reshape(seq_count // group, group, mesh.shape["head"]), ("zs", "slab", "head")
    )
    rows = P(SEQ, "head")
    placed = (rows, rows, rows, rows, P("head"), P(SEQ))
    return jax.shard_map(
        on_device,
        mesh=slabbed,
        in_specs=placed,
        out_specs=(rows, rows, rows, rows),
        check_vma=False,
    )
```

```python
import jax
import jax.numpy as jnp
from jax import lax
from jax.sharding import Mesh
from jax.sharding import PartitionSpec as P

DH = 128
WIDTH = 8192
SEQ = ("zs", "slab")
SLAB = 16


def causal_scores(left_rows, right_rows, causal):
    scores = jnp.einsum("thd,shd->hts", left_rows, right_rows, preferred_element_type=jnp.float32)
    return jnp.where(causal[None], scores, 0.0).astype(jnp.bfloat16)


def weighted_sum(weights, pieces):
    return jnp.sum(weights[:, :, None, None] * pieces[None], axis=1)


def shifted(value, axis, by):
    peers = lax.axis_size(axis)
    pairs = [(i, i + by) for i in range(peers) if 0 <= i + by < peers]
    return lax.ppermute(value, axis, pairs)


def with_rows(state, values):
    rows = jnp.zeros((state.shape[0], 8, state.shape[2]), jnp.float32)
    rows = rows.at[:, : values.shape[0], :].set(values.astype(jnp.float32)[None, :, None])
    return jnp.concatenate([state, rows], axis=1)


def forward_prefix(local_state, head_start, last_start, tokens_here):
    slabs = lax.axis_size("zs")
    group = lax.axis_size("slab")
    slab_index = lax.axis_index("zs")
    slab_first = slab_index * group
    blocks = slab_first + jnp.arange(group, dtype=jnp.int32)
    heads, rows, lanes = local_state.shape
    width = heads * rows // group
    payload = with_rows(local_state.reshape(group, width, lanes), jnp.stack([head_start, last_start]))
    arrived = lax.all_to_all(payload, "slab", 0, 0, tiled=True)
    pieces = arrived[:, :width]
    lows = arrived[:, width, 0].astype(jnp.int32) // tokens_here
    tail_low = arrived[group - 1, width + 1, 0].astype(jnp.int32) // tokens_here
    inner = (blocks[None, :] < blocks[:, None]) & (blocks[None, :] >= lows[:, None])
    in_slab = weighted_sum(inner.astype(jnp.float32), pieces)
    keep = blocks >= tail_low
    aggregate = jnp.sum(keep.astype(jnp.float32)[:, None, None] * pieces, axis=0)
    everyone = lax.all_to_all(
        jnp.broadcast_to(aggregate[None], (slabs,) + aggregate.shape), "zs", 0, 0, tiled=True
    )
    slab_ids = jnp.arange(slabs, dtype=jnp.int32)
    take = (slab_ids < slab_index) & (slab_ids >= lows[0] // group)
    earlier = jnp.sum(take.astype(jnp.float32)[:, None, None] * everyone, axis=0)
    reaches = (lows < slab_first).astype(jnp.float32)[:, None, None]
    prefix = in_slab + reaches * earlier[None]
    prefix = lax.all_to_all(prefix, "slab", 0, 0, tiled=True).reshape(heads, rows, lanes)
    return prefix, lows


def backward_suffix(local_state, lows):
    slabs = lax.axis_size("zs")
    group = lax.axis_size("slab")
    slab_index = lax.axis_index("zs")
    slab_first = slab_index * group
    blocks = slab_first + jnp.arange(group, dtype=jnp.int32)
    heads, rows, lanes = local_state.shape
    pieces = local_state.reshape(group, heads * rows // group, lanes)
    pieces = lax.all_to_all(pieces, "slab", 0, 0, tiled=True)
    inner = (blocks[None, :] > blocks[:, None]) & (lows[None, :] <= blocks[:, None])
    in_slab = weighted_sum(inner.astype(jnp.float32), pieces)
    keep = lows < slab_first
    aggregate = jnp.sum(keep.astype(jnp.float32)[:, None, None] * pieces, axis=0)
    width = aggregate.shape[0]
    sent = with_rows(aggregate[None], lows[0:1])[0]
    everyone = lax.all_to_all(
        jnp.broadcast_to(sent[None], (slabs,) + sent.shape), "zs", 0, 0, tiled=True
    )
    slab_ids = jnp.arange(slabs, dtype=jnp.int32)
    slab_lows = everyone[:, width, 0].astype(jnp.int32)
    take = (slab_ids[None, :] > slab_index) & (slab_lows[None, :] <= blocks[:, None])
    later = weighted_sum(take.astype(jnp.float32), everyone[:, :width])
    suffix = in_slab + later
    return lax.all_to_all(suffix, "slab", 0, 0, tiled=True).reshape(heads, rows, lanes)


def on_device(query_rows, key_rows, value_rows, grad_rows, norm_gain, doc_start):
    tokens_here = query_rows.shape[0]
    heads_here = query_rows.shape[1] // DH
    block_shape = (tokens_here, heads_here, DH)
    queries = query_rows.reshape(block_shape)
    key_vecs = key_rows.reshape(block_shape)
    value_vecs = value_rows.reshape(block_shape)
    grad_vecs = grad_rows.reshape(block_shape)
    gain_rows = norm_gain.astype(jnp.float32).reshape(heads_here, DH)
    block = lax.axis_index("zs") * lax.axis_size("slab") + lax.axis_index("slab")
    anchor = block * tokens_here
    positions = jnp.arange(tokens_here, dtype=jnp.int32)
    causal = (doc_start[:, None] == doc_start[None, :]) & (positions[None, :] <= positions[:, None])
    last_start = doc_start[-1]
    head_start = doc_start[0]
    block_count = lax.axis_size(SEQ)
    next_head = shifted(head_start, SEQ, -1)
    mask_last = (doc_start == last_start).astype(jnp.bfloat16)[:, None, None]
    local_state = jnp.einsum(
        "thd,the->hde", key_vecs * mask_last, value_vecs, preferred_element_type=jnp.float32
    )
    opens_before = (head_start < anchor).astype(jnp.float32)
    prefix, lows = forward_prefix(local_state, head_start, last_start, tokens_here)
    prefix_low = (prefix * opens_before).astype(jnp.bfloat16)
    mask_first = (doc_start < anchor).astype(jnp.float32)[:, None, None]
    weights = causal_scores(queries, key_vecs, causal)
    outputs = jnp.einsum("hts,she->the", weights, value_vecs, preferred_element_type=jnp.float32)
    outputs = outputs + mask_first * jnp.einsum(
        "thd,hde->the", queries, prefix_low, preferred_element_type=jnp.float32
    )
    scaled = grad_vecs.astype(jnp.float32) * gain_rows
    totals = lax.psum(
        (jnp.sum(outputs * outputs, axis=(1, 2)), jnp.sum(scaled * outputs, axis=(1, 2))), "head"
    )
    inv_rms = lax.rsqrt(totals[0] / WIDTH + 1e-06)
    normed = (outputs * inv_rms[:, None, None] * gain_rows).astype(jnp.bfloat16)
    grad_out = (
        inv_rms[:, None, None]
        * (scaled - outputs * (totals[1] * inv_rms * inv_rms / WIDTH)[:, None, None])
    ).astype(jnp.bfloat16)
    back_weights = causal_scores(grad_out, value_vecs, causal)
    grad_query = jnp.einsum(
        "hts,shd->thd", back_weights, key_vecs, preferred_element_type=jnp.float32
    )
    grad_query = grad_query + mask_first * jnp.einsum(
        "the,hde->thd", grad_out, prefix_low, preferred_element_type=jnp.float32
    )
    mask_head = (doc_start == head_start).astype(jnp.bfloat16)[:, None, None]
    back_state = jnp.einsum(
        "thd,the->hde", queries * mask_head, grad_out, preferred_element_type=jnp.float32
    )
    continues = (next_head // tokens_here <= block) & (block + 1 < block_count)
    suffix = backward_suffix(back_state, lows) * continues.astype(jnp.float32)
    suffix_low = suffix.astype(jnp.bfloat16)
    mask_tail = mask_last.astype(jnp.float32)
    grad_key = jnp.einsum("hts,thd->shd", back_weights, queries, preferred_element_type=jnp.float32)
    grad_key = grad_key + mask_tail * jnp.einsum(
        "she,hde->shd", value_vecs, suffix_low, preferred_element_type=jnp.float32
    )
    grad_value = jnp.einsum("hts,the->she", weights, grad_out, preferred_element_type=jnp.float32)
    grad_value = grad_value + mask_tail * jnp.einsum(
        "shd,hde->she", key_vecs, suffix_low, preferred_element_type=jnp.float32
    )
    flat = (tokens_here, heads_here * DH)
    return (
        normed.reshape(flat),
        grad_query.astype(jnp.bfloat16).reshape(flat),
        grad_key.astype(jnp.bfloat16).reshape(flat),
        grad_value.astype(jnp.bfloat16).reshape(flat),
    )


def solution(mesh):
    seq_count = mesh.shape["seq"]
    group = SLAB if seq_count % SLAB == 0 else 1
    slabbed = Mesh(
        mesh.devices.reshape(seq_count // group, group, mesh.shape["head"]), ("zs", "slab", "head")
    )
    rows = P(SEQ, "head")
    placed = (rows, rows, rows, rows, P("head"), P(SEQ))
    return jax.shard_map(
        on_device,
        mesh=slabbed,
        in_specs=placed,
        out_specs=(rows, rows, rows, rows),
        check_vma=False,
    )
```

```python
import jax
import jax.numpy as jnp
from jax import lax
from jax.sharding import Mesh
from jax.sharding import PartitionSpec as P

DH = 128
WIDTH = 8192
SEQ = ("zs", "slab")
SLAB = 16


def causal_scores(left_rows, right_rows, causal):
    scores = jnp.einsum("thd,shd->hts", left_rows, right_rows, preferred_element_type=jnp.float32)
    return jnp.where(causal[None], scores, 0.0).astype(jnp.bfloat16)


def weighted_sum(weights, pieces):
    return jnp.sum(weights[:, :, None, None] * pieces[None], axis=1)


def shifted(value, axis, by):
    peers = lax.axis_size(axis)
    pairs = [(i, i + by) for i in range(peers) if 0 <= i + by < peers]
    return lax.ppermute(value, axis, pairs)


def head_total(partial):
    peers = lax.axis_size("head")
    everyone = lax.all_to_all(
        jnp.broadcast_to(partial[None], (peers,) + partial.shape), "head", 0, 0, tiled=True
    )
    return jnp.sum(everyone, axis=0)


def with_rows(state, values):
    rows = jnp.zeros((state.shape[0], 8, state.shape[2]), jnp.float32)
    rows = rows.at[:, : values.shape[0], :].set(values.astype(jnp.float32)[None, :, None])
    return jnp.concatenate([state, rows], axis=1)


def forward_prefix(local_state, head_start, last_start, tokens_here):
    slabs = lax.axis_size("zs")
    group = lax.axis_size("slab")
    slab_index = lax.axis_index("zs")
    slab_first = slab_index * group
    blocks = slab_first + jnp.arange(group, dtype=jnp.int32)
    heads, rows, lanes = local_state.shape
    width = heads * rows // group
    payload = with_rows(local_state.reshape(group, width, lanes), jnp.stack([head_start, last_start]))
    arrived = lax.all_to_all(payload, "slab", 0, 0, tiled=True)
    pieces = arrived[:, :width]
    lows = arrived[:, width, 0].astype(jnp.int32) // tokens_here
    tail_low = arrived[group - 1, width + 1, 0].astype(jnp.int32) // tokens_here
    inner = (blocks[None, :] < blocks[:, None]) & (blocks[None, :] >= lows[:, None])
    in_slab = weighted_sum(inner.astype(jnp.float32), pieces)
    keep = blocks >= tail_low
    aggregate = jnp.sum(keep.astype(jnp.float32)[:, None, None] * pieces, axis=0)
    everyone = lax.all_to_all(
        jnp.broadcast_to(aggregate[None], (slabs,) + aggregate.shape), "zs", 0, 0, tiled=True
    )
    slab_ids = jnp.arange(slabs, dtype=jnp.int32)
    take = (slab_ids < slab_index) & (slab_ids >= lows[0] // group)
    earlier = jnp.sum(take.astype(jnp.float32)[:, None, None] * everyone, axis=0)
    reaches = (lows < slab_first).astype(jnp.float32)[:, None, None]
    prefix = in_slab + reaches * earlier[None]
    prefix = lax.all_to_all(prefix, "slab", 0, 0, tiled=True).reshape(heads, rows, lanes)
    return prefix, lows


def backward_suffix(local_state, lows):
    slabs = lax.axis_size("zs")
    group = lax.axis_size("slab")
    slab_index = lax.axis_index("zs")
    slab_first = slab_index * group
    blocks = slab_first + jnp.arange(group, dtype=jnp.int32)
    heads, rows, lanes = local_state.shape
    pieces = local_state.reshape(group, heads * rows // group, lanes)
    pieces = lax.all_to_all(pieces, "slab", 0, 0, tiled=True)
    inner = (blocks[None, :] > blocks[:, None]) & (lows[None, :] <= blocks[:, None])
    in_slab = weighted_sum(inner.astype(jnp.float32), pieces)
    keep = lows < slab_first
    aggregate = jnp.sum(keep.astype(jnp.float32)[:, None, None] * pieces, axis=0)
    width = aggregate.shape[0]
    sent = with_rows(aggregate[None], lows[0:1])[0]
    everyone = lax.all_to_all(
        jnp.broadcast_to(sent[None], (slabs,) + sent.shape), "zs", 0, 0, tiled=True
    )
    slab_ids = jnp.arange(slabs, dtype=jnp.int32)
    slab_lows = everyone[:, width, 0].astype(jnp.int32)
    take = (slab_ids[None, :] > slab_index) & (slab_lows[None, :] <= blocks[:, None])
    later = weighted_sum(take.astype(jnp.float32), everyone[:, :width])
    suffix = in_slab + later
    return lax.all_to_all(suffix, "slab", 0, 0, tiled=True).reshape(heads, rows, lanes)


def on_device(query_rows, key_rows, value_rows, grad_rows, norm_gain, doc_start):
    tokens_here = query_rows.shape[0]
    heads_here = query_rows.shape[1] // DH
    block_shape = (tokens_here, heads_here, DH)
    queries = query_rows.reshape(block_shape)
    key_vecs = key_rows.reshape(block_shape)
    value_vecs = value_rows.reshape(block_shape)
    grad_vecs = grad_rows.reshape(block_shape)
    gain_rows = norm_gain.astype(jnp.float32).reshape(heads_here, DH)
    block = lax.axis_index("zs") * lax.axis_size("slab") + lax.axis_index("slab")
    anchor = block * tokens_here
    positions = jnp.arange(tokens_here, dtype=jnp.int32)
    causal = (doc_start[:, None] == doc_start[None, :]) & (positions[None, :] <= positions[:, None])
    last_start = doc_start[-1]
    head_start = doc_start[0]
    block_count = lax.axis_size(SEQ)
    next_head = shifted(head_start, SEQ, -1)
    mask_last = (doc_start == last_start).astype(jnp.bfloat16)[:, None, None]
    local_state = jnp.einsum(
        "thd,the->hde", key_vecs * mask_last, value_vecs, preferred_element_type=jnp.float32
    )
    opens_before = (head_start < anchor).astype(jnp.float32)
    prefix, lows = forward_prefix(local_state, head_start, last_start, tokens_here)
    prefix_low = (prefix * opens_before).astype(jnp.bfloat16)
    mask_first = (doc_start < anchor).astype(jnp.float32)[:, None, None]
    weights = causal_scores(queries, key_vecs, causal)
    outputs = jnp.einsum("hts,she->the", weights, value_vecs, preferred_element_type=jnp.float32)
    outputs = outputs + mask_first * jnp.einsum(
        "thd,hde->the", queries, prefix_low, preferred_element_type=jnp.float32
    )
    scaled = grad_vecs.astype(jnp.float32) * gain_rows
    totals = head_total(
        jnp.stack([jnp.sum(outputs * outputs, axis=(1, 2)), jnp.sum(scaled * outputs, axis=(1, 2))])
    )
    inv_rms = lax.rsqrt(totals[0] / WIDTH + 1e-06)
    normed = (outputs * inv_rms[:, None, None] * gain_rows).astype(jnp.bfloat16)
    grad_out = (
        inv_rms[:, None, None]
        * (scaled - outputs * (totals[1] * inv_rms * inv_rms / WIDTH)[:, None, None])
    ).astype(jnp.bfloat16)
    back_weights = causal_scores(grad_out, value_vecs, causal)
    grad_query = jnp.einsum(
        "hts,shd->thd", back_weights, key_vecs, preferred_element_type=jnp.float32
    )
    grad_query = grad_query + mask_first * jnp.einsum(
        "the,hde->thd", grad_out, prefix_low, preferred_element_type=jnp.float32
    )
    mask_head = (doc_start == head_start).astype(jnp.bfloat16)[:, None, None]
    back_state = jnp.einsum(
        "thd,the->hde", queries * mask_head, grad_out, preferred_element_type=jnp.float32
    )
    continues = (next_head // tokens_here <= block) & (block + 1 < block_count)
    suffix = backward_suffix(back_state, lows) * continues.astype(jnp.float32)
    suffix_low = suffix.astype(jnp.bfloat16)
    mask_tail = mask_last.astype(jnp.float32)
    grad_key = jnp.einsum("hts,thd->shd", back_weights, queries, preferred_element_type=jnp.float32)
    grad_key = grad_key + mask_tail * jnp.einsum(
        "she,hde->shd", value_vecs, suffix_low, preferred_element_type=jnp.float32
    )
    grad_value = jnp.einsum("hts,the->she", weights, grad_out, preferred_element_type=jnp.float32)
    grad_value = grad_value + mask_tail * jnp.einsum(
        "shd,hde->she", key_vecs, suffix_low, preferred_element_type=jnp.float32
    )
    flat = (tokens_here, heads_here * DH)
    return (
        normed.reshape(flat),
        grad_query.astype(jnp.bfloat16).reshape(flat),
        grad_key.astype(jnp.bfloat16).reshape(flat),
        grad_value.astype(jnp.bfloat16).reshape(flat),
    )


def solution(mesh):
    seq_count = mesh.shape["seq"]
    group = SLAB if seq_count % SLAB == 0 else 1
    slabbed = Mesh(
        mesh.devices.reshape(seq_count // group, group, mesh.shape["head"]), ("zs", "slab", "head")
    )
    rows = P(SEQ, "head")
    placed = (rows, rows, rows, rows, P("head"), P(SEQ))
    return jax.shard_map(
        on_device,
        mesh=slabbed,
        in_specs=placed,
        out_specs=(rows, rows, rows, rows),
        check_vma=False,
    )
```

```python
import jax
import jax.numpy as jnp
from jax import lax
from jax.sharding import Mesh
from jax.sharding import PartitionSpec as P

DH = 128
WIDTH = 8192
SEQ = ("zs", "slab")
SLAB = 8


def causal_scores(left_rows, right_rows, causal):
    scores = jnp.einsum("thd,shd->hts", left_rows, right_rows, preferred_element_type=jnp.float32)
    return jnp.where(causal[None], scores, 0.0).astype(jnp.bfloat16)


def weighted_sum(weights, pieces):
    return jnp.sum(weights[:, :, None, None] * pieces[None], axis=1)


def shifted(value, axis, by):
    peers = lax.axis_size(axis)
    pairs = [(i, i + by) for i in range(peers) if 0 <= i + by < peers]
    return lax.ppermute(value, axis, pairs)


def head_total(partial):
    peers = lax.axis_size("head")
    everyone = lax.all_to_all(
        jnp.broadcast_to(partial[None], (peers,) + partial.shape), "head", 0, 0, tiled=True
    )
    return jnp.sum(everyone, axis=0)


def with_rows(state, values):
    rows = jnp.zeros((state.shape[0], 8, state.shape[2]), jnp.float32)
    rows = rows.at[:, : values.shape[0], :].set(values.astype(jnp.float32)[None, :, None])
    return jnp.concatenate([state, rows], axis=1)


def forward_prefix(local_state, head_start, last_start, tokens_here):
    slabs = lax.axis_size("zs")
    group = lax.axis_size("slab")
    slab_index = lax.axis_index("zs")
    slab_first = slab_index * group
    blocks = slab_first + jnp.arange(group, dtype=jnp.int32)
    heads, rows, lanes = local_state.shape
    width = heads * rows // group
    payload = with_rows(local_state.reshape(group, width, lanes), jnp.stack([head_start, last_start]))
    arrived = lax.all_to_all(payload, "slab", 0, 0, tiled=True)
    pieces = arrived[:, :width]
    lows = arrived[:, width, 0].astype(jnp.int32) // tokens_here
    tail_low = arrived[group - 1, width + 1, 0].astype(jnp.int32) // tokens_here
    inner = (blocks[None, :] < blocks[:, None]) & (blocks[None, :] >= lows[:, None])
    in_slab = weighted_sum(inner.astype(jnp.float32), pieces)
    keep = blocks >= tail_low
    aggregate = jnp.sum(keep.astype(jnp.float32)[:, None, None] * pieces, axis=0)
    everyone = lax.all_to_all(
        jnp.broadcast_to(aggregate[None], (slabs,) + aggregate.shape), "zs", 0, 0, tiled=True
    )
    slab_ids = jnp.arange(slabs, dtype=jnp.int32)
    take = (slab_ids < slab_index) & (slab_ids >= lows[0] // group)
    earlier = jnp.sum(take.astype(jnp.float32)[:, None, None] * everyone, axis=0)
    reaches = (lows < slab_first).astype(jnp.float32)[:, None, None]
    prefix = in_slab + reaches * earlier[None]
    prefix = lax.all_to_all(prefix, "slab", 0, 0, tiled=True).reshape(heads, rows, lanes)
    return prefix, lows


def backward_suffix(local_state, lows):
    slabs = lax.axis_size("zs")
    group = lax.axis_size("slab")
    slab_index = lax.axis_index("zs")
    slab_first = slab_index * group
    blocks = slab_first + jnp.arange(group, dtype=jnp.int32)
    heads, rows, lanes = local_state.shape
    pieces = local_state.reshape(group, heads * rows // group, lanes)
    pieces = lax.all_to_all(pieces, "slab", 0, 0, tiled=True)
    inner = (blocks[None, :] > blocks[:, None]) & (lows[None, :] <= blocks[:, None])
    in_slab = weighted_sum(inner.astype(jnp.float32), pieces)
    keep = lows < slab_first
    aggregate = jnp.sum(keep.astype(jnp.float32)[:, None, None] * pieces, axis=0)
    width = aggregate.shape[0]
    sent = with_rows(aggregate[None], lows[0:1])[0]
    everyone = lax.all_to_all(
        jnp.broadcast_to(sent[None], (slabs,) + sent.shape), "zs", 0, 0, tiled=True
    )
    slab_ids = jnp.arange(slabs, dtype=jnp.int32)
    slab_lows = everyone[:, width, 0].astype(jnp.int32)
    take = (slab_ids[None, :] > slab_index) & (slab_lows[None, :] <= blocks[:, None])
    later = weighted_sum(take.astype(jnp.float32), everyone[:, :width])
    suffix = in_slab + later
    return lax.all_to_all(suffix, "slab", 0, 0, tiled=True).reshape(heads, rows, lanes)


def on_device(query_rows, key_rows, value_rows, grad_rows, norm_gain, doc_start):
    tokens_here = query_rows.shape[0]
    heads_here = query_rows.shape[1] // DH
    block_shape = (tokens_here, heads_here, DH)
    queries = query_rows.reshape(block_shape)
    key_vecs = key_rows.reshape(block_shape)
    value_vecs = value_rows.reshape(block_shape)
    grad_vecs = grad_rows.reshape(block_shape)
    gain_rows = norm_gain.astype(jnp.float32).reshape(heads_here, DH)
    block = lax.axis_index("zs") * lax.axis_size("slab") + lax.axis_index("slab")
    anchor = block * tokens_here
    positions = jnp.arange(tokens_here, dtype=jnp.int32)
    causal = (doc_start[:, None] == doc_start[None, :]) & (positions[None, :] <= positions[:, None])
    last_start = doc_start[-1]
    head_start = doc_start[0]
    block_count = lax.axis_size(SEQ)
    next_head = shifted(head_start, SEQ, -1)
    mask_last = (doc_start == last_start).astype(jnp.bfloat16)[:, None, None]
    local_state = jnp.einsum(
        "thd,the->hde", key_vecs * mask_last, value_vecs, preferred_element_type=jnp.float32
    )
    opens_before = (head_start < anchor).astype(jnp.float32)
    prefix, lows = forward_prefix(local_state, head_start, last_start, tokens_here)
    prefix_low = (prefix * opens_before).astype(jnp.bfloat16)
    mask_first = (doc_start < anchor).astype(jnp.float32)[:, None, None]
    weights = causal_scores(queries, key_vecs, causal)
    outputs = jnp.einsum("hts,she->the", weights, value_vecs, preferred_element_type=jnp.float32)
    outputs = outputs + mask_first * jnp.einsum(
        "thd,hde->the", queries, prefix_low, preferred_element_type=jnp.float32
    )
    scaled = grad_vecs.astype(jnp.float32) * gain_rows
    totals = head_total(
        jnp.stack([jnp.sum(outputs * outputs, axis=(1, 2)), jnp.sum(scaled * outputs, axis=(1, 2))])
    )
    inv_rms = lax.rsqrt(totals[0] / WIDTH + 1e-06)
    normed = (outputs * inv_rms[:, None, None] * gain_rows).astype(jnp.bfloat16)
    grad_out = (
        inv_rms[:, None, None]
        * (scaled - outputs * (totals[1] * inv_rms * inv_rms / WIDTH)[:, None, None])
    ).astype(jnp.bfloat16)
    back_weights = causal_scores(grad_out, value_vecs, causal)
    grad_query = jnp.einsum(
        "hts,shd->thd", back_weights, key_vecs, preferred_element_type=jnp.float32
    )
    grad_query = grad_query + mask_first * jnp.einsum(
        "the,hde->thd", grad_out, prefix_low, preferred_element_type=jnp.float32
    )
    mask_head = (doc_start == head_start).astype(jnp.bfloat16)[:, None, None]
    back_state = jnp.einsum(
        "thd,the->hde", queries * mask_head, grad_out, preferred_element_type=jnp.float32
    )
    continues = (next_head // tokens_here <= block) & (block + 1 < block_count)
    suffix = backward_suffix(back_state, lows) * continues.astype(jnp.float32)
    suffix_low = suffix.astype(jnp.bfloat16)
    mask_tail = mask_last.astype(jnp.float32)
    grad_key = jnp.einsum("hts,thd->shd", back_weights, queries, preferred_element_type=jnp.float32)
    grad_key = grad_key + mask_tail * jnp.einsum(
        "she,hde->shd", value_vecs, suffix_low, preferred_element_type=jnp.float32
    )
    grad_value = jnp.einsum("hts,the->she", weights, grad_out, preferred_element_type=jnp.float32)
    grad_value = grad_value + mask_tail * jnp.einsum(
        "shd,hde->she", key_vecs, suffix_low, preferred_element_type=jnp.float32
    )
    flat = (tokens_here, heads_here * DH)
    return (
        normed.reshape(flat),
        grad_query.astype(jnp.bfloat16).reshape(flat),
        grad_key.astype(jnp.bfloat16).reshape(flat),
        grad_value.astype(jnp.bfloat16).reshape(flat),
    )


def solution(mesh):
    seq_count = mesh.shape["seq"]
    group = SLAB if seq_count % SLAB == 0 else 1
    slabbed = Mesh(
        mesh.devices.reshape(seq_count // group, group, mesh.shape["head"]), ("zs", "slab", "head")
    )
    rows = P(SEQ, "head")
    placed = (rows, rows, rows, rows, P("head"), P(SEQ))
    return jax.shard_map(
        on_device,
        mesh=slabbed,
        in_specs=placed,
        out_specs=(rows, rows, rows, rows),
        check_vma=False,
    )
```

```python
import jax
import jax.numpy as jnp
from jax import lax
from jax.sharding import Mesh
from jax.sharding import PartitionSpec as P

DH = 128
WIDTH = 8192
SEQ = ("zs", "slab")
SLAB = 16


def causal_scores(left_rows, right_rows, causal):
    scores = jnp.einsum("thd,shd->hts", left_rows, right_rows, preferred_element_type=jnp.float32)
    return jnp.where(causal[None], scores, 0.0).astype(jnp.bfloat16)


def weighted_sum(weights, pieces):
    return jnp.sum(weights[:, :, None, None] * pieces[None], axis=1)


def head_total(partial):
    peers = lax.axis_size("head")
    everyone = lax.all_to_all(
        jnp.broadcast_to(partial[None], (peers,) + partial.shape), "head", 0, 0, tiled=True
    )
    return jnp.sum(everyone, axis=0)


def with_rows(state, values):
    rows = jnp.zeros((state.shape[0], 8, state.shape[2]), jnp.float32)
    rows = rows.at[:, : values.shape[0], :].set(values.astype(jnp.float32)[None, :, None])
    return jnp.concatenate([state, rows], axis=1)


def forward_prefix(local_state, doc_start, tokens_here):
    slabs = lax.axis_size("zs")
    group = lax.axis_size("slab")
    slab_index = lax.axis_index("zs")
    slab_first = slab_index * group
    blocks = slab_first + jnp.arange(group, dtype=jnp.int32)
    heads, rows, lanes = local_state.shape
    width = heads * rows // group
    starts_row = jnp.zeros((group, 8, lanes), jnp.float32)
    starts_row = starts_row.at[:, 0, :].set(doc_start.astype(jnp.float32)[None, :])
    payload = jnp.concatenate([local_state.reshape(group, width, lanes), starts_row], axis=1)
    arrived = lax.all_to_all(payload, "slab", 0, 0, tiled=True)
    pieces = arrived[:, :width]
    lows = arrived[:, width, 0].astype(jnp.int32) // tokens_here
    tail_low = arrived[group - 1, width, lanes - 1].astype(jnp.int32) // tokens_here
    inner = (blocks[None, :] < blocks[:, None]) & (blocks[None, :] >= lows[:, None])
    in_slab = weighted_sum(inner.astype(jnp.float32), pieces)
    keep = blocks >= tail_low
    aggregate = jnp.sum(keep.astype(jnp.float32)[:, None, None] * pieces, axis=0)
    everyone = lax.all_to_all(
        jnp.broadcast_to(aggregate[None], (slabs,) + aggregate.shape), "zs", 0, 0, tiled=True
    )
    slab_ids = jnp.arange(slabs, dtype=jnp.int32)
    take = (slab_ids < slab_index) & (slab_ids >= lows[0] // group)
    earlier = jnp.sum(take.astype(jnp.float32)[:, None, None] * everyone, axis=0)
    reaches = (lows < slab_first).astype(jnp.float32)[:, None, None]
    prefix = in_slab + reaches * earlier[None]
    prefix = lax.all_to_all(prefix, "slab", 0, 0, tiled=True).reshape(heads, rows, lanes)
    return prefix, lows


def backward_suffix(local_state, lows):
    slabs = lax.axis_size("zs")
    group = lax.axis_size("slab")
    slab_index = lax.axis_index("zs")
    slab_first = slab_index * group
    blocks = slab_first + jnp.arange(group, dtype=jnp.int32)
    heads, rows, lanes = local_state.shape
    pieces = local_state.reshape(group, heads * rows // group, lanes)
    pieces = lax.all_to_all(pieces, "slab", 0, 0, tiled=True)
    inner = (blocks[None, :] > blocks[:, None]) & (lows[None, :] <= blocks[:, None])
    in_slab = weighted_sum(inner.astype(jnp.float32), pieces)
    keep = lows < slab_first
    aggregate = jnp.sum(keep.astype(jnp.float32)[:, None, None] * pieces, axis=0)
    width = aggregate.shape[0]
    sent = with_rows(aggregate[None], lows[0:1])[0]
    everyone = lax.all_to_all(
        jnp.broadcast_to(sent[None], (slabs,) + sent.shape), "zs", 0, 0, tiled=True
    )
    slab_ids = jnp.arange(slabs, dtype=jnp.int32)
    slab_lows = everyone[:, width, 0].astype(jnp.int32)
    take = (slab_ids[None, :] > slab_index) & (slab_lows[None, :] <= blocks[:, None])
    later = weighted_sum(take.astype(jnp.float32), everyone[:, :width])
    suffix = in_slab + later
    next_slab_low = slab_lows[jnp.minimum(slab_index + 1, slabs - 1)]
    suffix = lax.all_to_all(suffix, "slab", 0, 0, tiled=True).reshape(heads, rows, lanes)
    return suffix, next_slab_low


def on_device(query_rows, key_rows, value_rows, grad_rows, norm_gain, doc_start):
    tokens_here = query_rows.shape[0]
    heads_here = query_rows.shape[1] // DH
    block_shape = (tokens_here, heads_here, DH)
    queries = query_rows.reshape(block_shape)
    key_vecs = key_rows.reshape(block_shape)
    value_vecs = value_rows.reshape(block_shape)
    grad_vecs = grad_rows.reshape(block_shape)
    gain_rows = norm_gain.astype(jnp.float32).reshape(heads_here, DH)
    block = lax.axis_index("zs") * lax.axis_size("slab") + lax.axis_index("slab")
    anchor = block * tokens_here
    positions = jnp.arange(tokens_here, dtype=jnp.int32)
    causal = (doc_start[:, None] == doc_start[None, :]) & (positions[None, :] <= positions[:, None])
    last_start = doc_start[-1]
    head_start = doc_start[0]
    block_count = lax.axis_size(SEQ)
    mask_last = (doc_start == last_start).astype(jnp.bfloat16)[:, None, None]
    local_state = jnp.einsum(
        "thd,the->hde", key_vecs * mask_last, value_vecs, preferred_element_type=jnp.float32
    )
    opens_before = (head_start < anchor).astype(jnp.float32)
    prefix, lows = forward_prefix(local_state, doc_start, tokens_here)
    prefix_low = (prefix * opens_before).astype(jnp.bfloat16)
    mask_first = (doc_start < anchor).astype(jnp.float32)[:, None, None]
    weights = causal_scores(queries, key_vecs, causal)
    outputs = jnp.einsum("hts,she->the", weights, value_vecs, preferred_element_type=jnp.float32)
    outputs = outputs + mask_first * jnp.einsum(
        "thd,hde->the", queries, prefix_low, preferred_element_type=jnp.float32
    )
    scaled = grad_vecs.astype(jnp.float32) * gain_rows
    totals = head_total(
        jnp.stack([jnp.sum(outputs * outputs, axis=(1, 2)), jnp.sum(scaled * outputs, axis=(1, 2))])
    )
    inv_rms = lax.rsqrt(totals[0] / WIDTH + 1e-06)
    normed = (outputs * inv_rms[:, None, None] * gain_rows).astype(jnp.bfloat16)
    grad_out = (
        inv_rms[:, None, None]
        * (scaled - outputs * (totals[1] * inv_rms * inv_rms / WIDTH)[:, None, None])
    ).astype(jnp.bfloat16)
    back_weights = causal_scores(grad_out, value_vecs, causal)
    grad_query = jnp.einsum(
        "hts,shd->thd", back_weights, key_vecs, preferred_element_type=jnp.float32
    )
    grad_query = grad_query + mask_first * jnp.einsum(
        "the,hde->thd", grad_out, prefix_low, preferred_element_type=jnp.float32
    )
    mask_head = (doc_start == head_start).astype(jnp.bfloat16)[:, None, None]
    back_state = jnp.einsum(
        "thd,the->hde", queries * mask_head, grad_out, preferred_element_type=jnp.float32
    )
    suffix, next_slab_low = backward_suffix(back_state, lows)
    place = lax.axis_index("slab")
    group = lows.shape[0]
    next_low = jnp.where(place + 1 < group, lows[jnp.minimum(place + 1, group - 1)], next_slab_low)
    continues = (next_low <= block) & (block + 1 < block_count)
    suffix = suffix * continues.astype(jnp.float32)
    suffix_low = suffix.astype(jnp.bfloat16)
    mask_tail = mask_last.astype(jnp.float32)
    grad_key = jnp.einsum("hts,thd->shd", back_weights, queries, preferred_element_type=jnp.float32)
    grad_key = grad_key + mask_tail * jnp.einsum(
        "she,hde->shd", value_vecs, suffix_low, preferred_element_type=jnp.float32
    )
    grad_value = jnp.einsum("hts,the->she", weights, grad_out, preferred_element_type=jnp.float32)
    grad_value = grad_value + mask_tail * jnp.einsum(
        "shd,hde->she", key_vecs, suffix_low, preferred_element_type=jnp.float32
    )
    flat = (tokens_here, heads_here * DH)
    return (
        normed.reshape(flat),
        grad_query.astype(jnp.bfloat16).reshape(flat),
        grad_key.astype(jnp.bfloat16).reshape(flat),
        grad_value.astype(jnp.bfloat16).reshape(flat),
    )


def solution(mesh):
    seq_count = mesh.shape["seq"]
    group = SLAB if seq_count % SLAB == 0 else 1
    slabbed = Mesh(
        mesh.devices.reshape(seq_count // group, group, mesh.shape["head"]), ("zs", "slab", "head")
    )
    rows = P(SEQ, "head")
    placed = (rows, rows, rows, rows, P("head"), P(SEQ))
    return jax.shard_map(
        on_device,
        mesh=slabbed,
        in_specs=placed,
        out_specs=(rows, rows, rows, rows),
        check_vma=False,
    )
```

```python
import jax
import jax.numpy as jnp
from jax import lax
from jax.sharding import PartitionSpec as P

DH = 128
WIDTH = 8192
SEQ = "seq"


def causal_scores(left_rows, right_rows, causal):
    scores = jnp.einsum("thd,shd->hts", left_rows, right_rows, preferred_element_type=jnp.float32)
    return jnp.where(causal[None], scores, 0.0).astype(jnp.bfloat16)


def head_total(partial):
    peers = lax.axis_size("head")
    everyone = lax.all_to_all(
        jnp.broadcast_to(partial[None], (peers,) + partial.shape), "head", 0, 0, tiled=True
    )
    return jnp.sum(everyone, axis=0)


def to_pieces(state, peers, lanes):
    flat = state.reshape(-1)
    span = -(-flat.shape[0] // (peers * lanes)) * lanes
    flat = jnp.pad(flat, (0, peers * span - flat.shape[0]))
    return flat.reshape(peers, span)


def from_pieces(pieces, shape):
    size = shape[0] * shape[1] * shape[2]
    return pieces.reshape(-1)[:size].reshape(shape)


def mix(weights, pieces):
    return jnp.dot(weights, pieces, precision=lax.Precision.HIGHEST, preferred_element_type=jnp.float32)


def forward_prefix(local_state, doc_start, tokens_here):
    peers = lax.axis_size(SEQ)
    lanes = local_state.shape[-1]
    pieces = to_pieces(local_state, peers, lanes)
    span = pieces.shape[1]
    starts = jnp.broadcast_to(doc_start.astype(jnp.float32)[None], (peers, doc_start.shape[0]))
    arrived = lax.all_to_all(jnp.concatenate([pieces, starts], axis=1), SEQ, 0, 0, tiled=True)
    blocks = jnp.arange(peers, dtype=jnp.int32)
    lows = arrived[:, span].astype(jnp.int32) // tokens_here
    inner = (blocks[None, :] < blocks[:, None]) & (blocks[None, :] >= lows[:, None])
    prefix = mix(inner.astype(jnp.float32), arrived[:, :span])
    prefix = lax.all_to_all(prefix, SEQ, 0, 0, tiled=True)
    return from_pieces(prefix, local_state.shape), lows


def backward_suffix(local_state, lows):
    peers = lax.axis_size(SEQ)
    lanes = local_state.shape[-1]
    pieces = lax.all_to_all(to_pieces(local_state, peers, lanes), SEQ, 0, 0, tiled=True)
    blocks = jnp.arange(peers, dtype=jnp.int32)
    inner = (blocks[None, :] > blocks[:, None]) & (lows[None, :] <= blocks[:, None])
    suffix = mix(inner.astype(jnp.float32), pieces)
    suffix = lax.all_to_all(suffix, SEQ, 0, 0, tiled=True)
    return from_pieces(suffix, local_state.shape)


def on_device(query_rows, key_rows, value_rows, grad_rows, norm_gain, doc_start):
    tokens_here = query_rows.shape[0]
    heads_here = query_rows.shape[1] // DH
    block_shape = (tokens_here, heads_here, DH)
    queries = query_rows.reshape(block_shape)
    key_vecs = key_rows.reshape(block_shape)
    value_vecs = value_rows.reshape(block_shape)
    grad_vecs = grad_rows.reshape(block_shape)
    gain_rows = norm_gain.astype(jnp.float32).reshape(heads_here, DH)
    block = lax.axis_index(SEQ)
    anchor = block * tokens_here
    positions = jnp.arange(tokens_here, dtype=jnp.int32)
    causal = (doc_start[:, None] == doc_start[None, :]) & (positions[None, :] <= positions[:, None])
    last_start = doc_start[-1]
    head_start = doc_start[0]
    block_count = lax.axis_size(SEQ)
    mask_last = (doc_start == last_start).astype(jnp.bfloat16)[:, None, None]
    local_state = jnp.einsum(
        "thd,the->hde", key_vecs * mask_last, value_vecs, preferred_element_type=jnp.float32
    )
    opens_before = (head_start < anchor).astype(jnp.float32)
    prefix, lows = forward_prefix(local_state, doc_start, tokens_here)
    prefix_low = (prefix * opens_before).astype(jnp.bfloat16)
    mask_first = (doc_start < anchor).astype(jnp.float32)[:, None, None]
    weights = causal_scores(queries, key_vecs, causal)
    outputs = jnp.einsum("hts,she->the", weights, value_vecs, preferred_element_type=jnp.float32)
    outputs = outputs + mask_first * jnp.einsum(
        "thd,hde->the", queries, prefix_low, preferred_element_type=jnp.float32
    )
    scaled = grad_vecs.astype(jnp.float32) * gain_rows
    totals = head_total(
        jnp.stack([jnp.sum(outputs * outputs, axis=(1, 2)), jnp.sum(scaled * outputs, axis=(1, 2))])
    )
    inv_rms = lax.rsqrt(totals[0] / WIDTH + 1e-06)
    normed = (outputs * inv_rms[:, None, None] * gain_rows).astype(jnp.bfloat16)
    grad_out = (
        inv_rms[:, None, None]
        * (scaled - outputs * (totals[1] * inv_rms * inv_rms / WIDTH)[:, None, None])
    ).astype(jnp.bfloat16)
    back_weights = causal_scores(grad_out, value_vecs, causal)
    grad_query = jnp.einsum(
        "hts,shd->thd", back_weights, key_vecs, preferred_element_type=jnp.float32
    )
    grad_query = grad_query + mask_first * jnp.einsum(
        "the,hde->thd", grad_out, prefix_low, preferred_element_type=jnp.float32
    )
    mask_head = (doc_start == head_start).astype(jnp.bfloat16)[:, None, None]
    back_state = jnp.einsum(
        "thd,the->hde", queries * mask_head, grad_out, preferred_element_type=jnp.float32
    )
    suffix = backward_suffix(back_state, lows)
    next_low = lows[jnp.minimum(block + 1, block_count - 1)]
    continues = (next_low <= block) & (block + 1 < block_count)
    suffix = suffix * continues.astype(jnp.float32)
    suffix_low = suffix.astype(jnp.bfloat16)
    mask_tail = mask_last.astype(jnp.float32)
    grad_key = jnp.einsum("hts,thd->shd", back_weights, queries, preferred_element_type=jnp.float32)
    grad_key = grad_key + mask_tail * jnp.einsum(
        "she,hde->shd", value_vecs, suffix_low, preferred_element_type=jnp.float32
    )
    grad_value = jnp.einsum("hts,the->she", weights, grad_out, preferred_element_type=jnp.float32)
    grad_value = grad_value + mask_tail * jnp.einsum(
        "shd,hde->she", key_vecs, suffix_low, preferred_element_type=jnp.float32
    )
    flat = (tokens_here, heads_here * DH)
    return (
        normed.reshape(flat),
        grad_query.astype(jnp.bfloat16).reshape(flat),
        grad_key.astype(jnp.bfloat16).reshape(flat),
        grad_value.astype(jnp.bfloat16).reshape(flat),
    )


def solution(mesh):
    rows = P(SEQ, "head")
    placed = (rows, rows, rows, rows, P("head"), P(SEQ))
    return jax.shard_map(
        on_device,
        mesh=mesh,
        in_specs=placed,
        out_specs=(rows, rows, rows, rows),
        check_vma=False,
    )
```

```python
import jax
import jax.numpy as jnp
from jax import lax
from jax.sharding import Mesh
from jax.sharding import PartitionSpec as P

DH = 128
WIDTH = 8192
SEQ = ("zs", "slab")
SLAB = 16


def causal_scores(left_rows, right_rows, causal):
    scores = jnp.einsum("thd,shd->hts", left_rows, right_rows, preferred_element_type=jnp.float32)
    return jnp.where(causal[None], scores, 0.0).astype(jnp.bfloat16)


def weighted_sum(weights, pieces):
    return jnp.sum(weights[:, :, None, None] * pieces[None], axis=1)


def head_total(partial):
    peers = lax.axis_size("head")
    everyone = lax.all_to_all(
        jnp.broadcast_to(partial[None], (peers,) + partial.shape), "head", 0, 0, tiled=True
    )
    return jnp.sum(everyone, axis=0)


def with_rows(state, values):
    rows = jnp.zeros((state.shape[0], 8, state.shape[2]), jnp.float32)
    rows = rows.at[:, : values.shape[0], :].set(values.astype(jnp.float32)[None, :, None])
    return jnp.concatenate([state, rows], axis=1)


def forward_prefix(local_state, doc_start, tokens_here):
    slabs = lax.axis_size("zs")
    group = lax.axis_size("slab")
    slab_index = lax.axis_index("zs")
    slab_first = slab_index * group
    blocks = slab_first + jnp.arange(group, dtype=jnp.int32)
    heads, rows, lanes = local_state.shape
    width = heads * rows // group
    starts_row = jnp.zeros((group, 8, lanes), jnp.float32)
    starts_row = starts_row.at[:, 0, :].set(doc_start.astype(jnp.float32)[None, :])
    payload = jnp.concatenate([local_state.reshape(group, width, lanes), starts_row], axis=1)
    arrived = lax.all_to_all(payload, "slab", 0, 0, tiled=True)
    pieces = arrived[:, :width]
    lows = arrived[:, width, 0].astype(jnp.int32) // tokens_here
    tail_low = arrived[group - 1 :, width, lanes - 1].astype(jnp.int32) // tokens_here
    inner = (blocks[None, :] < blocks[:, None]) & (blocks[None, :] >= lows[:, None])
    in_slab = weighted_sum(inner.astype(jnp.float32), pieces)
    keep = blocks >= tail_low
    aggregate = jnp.sum(keep.astype(jnp.float32)[:, None, None] * pieces, axis=0)
    everyone = lax.all_to_all(
        jnp.broadcast_to(aggregate[None], (slabs,) + aggregate.shape), "zs", 0, 0, tiled=True
    )
    slab_ids = jnp.arange(slabs, dtype=jnp.int32)
    take = (slab_ids < slab_index) & (slab_ids >= lows[:1] // group)
    earlier = jnp.sum(take.astype(jnp.float32)[:, None, None] * everyone, axis=0)
    reaches = (lows < slab_first).astype(jnp.float32)[:, None, None]
    prefix = in_slab + reaches * earlier[None]
    prefix = lax.all_to_all(prefix, "slab", 0, 0, tiled=True).reshape(heads, rows, lanes)
    return prefix, lows


def backward_suffix(local_state, lows):
    slabs = lax.axis_size("zs")
    group = lax.axis_size("slab")
    slab_index = lax.axis_index("zs")
    slab_first = slab_index * group
    blocks = slab_first + jnp.arange(group, dtype=jnp.int32)
    heads, rows, lanes = local_state.shape
    pieces = local_state.reshape(group, heads * rows // group, lanes)
    pieces = lax.all_to_all(pieces, "slab", 0, 0, tiled=True)
    inner = (blocks[None, :] > blocks[:, None]) & (lows[None, :] <= blocks[:, None])
    in_slab = weighted_sum(inner.astype(jnp.float32), pieces)
    keep = lows < slab_first
    aggregate = jnp.sum(keep.astype(jnp.float32)[:, None, None] * pieces, axis=0)
    width = aggregate.shape[0]
    sent = with_rows(aggregate[None], lows[0:1])[0]
    everyone = lax.all_to_all(
        jnp.broadcast_to(sent[None], (slabs,) + sent.shape), "zs", 0, 0, tiled=True
    )
    slab_ids = jnp.arange(slabs, dtype=jnp.int32)
    slab_lows = everyone[:, width, 0].astype(jnp.int32)
    take = (slab_ids[None, :] > slab_index) & (slab_lows[None, :] <= blocks[:, None])
    later = weighted_sum(take.astype(jnp.float32), everyone[:, :width])
    suffix = in_slab + later
    next_slab_low = jnp.sum(jnp.where(slab_ids == slab_index + 1, slab_lows, 0))
    suffix = lax.all_to_all(suffix, "slab", 0, 0, tiled=True).reshape(heads, rows, lanes)
    return suffix, next_slab_low


def on_device(query_rows, key_rows, value_rows, grad_rows, norm_gain, doc_start):
    tokens_here = query_rows.shape[0]
    heads_here = query_rows.shape[1] // DH
    block_shape = (tokens_here, heads_here, DH)
    queries = query_rows.reshape(block_shape)
    key_vecs = key_rows.reshape(block_shape)
    value_vecs = value_rows.reshape(block_shape)
    grad_vecs = grad_rows.reshape(block_shape)
    gain_rows = norm_gain.astype(jnp.float32).reshape(heads_here, DH)
    block = lax.axis_index("zs") * lax.axis_size("slab") + lax.axis_index("slab")
    anchor = block * tokens_here
    positions = jnp.arange(tokens_here, dtype=jnp.int32)
    causal = (doc_start[:, None] == doc_start[None, :]) & (positions[None, :] <= positions[:, None])
    last_start = doc_start[-1]
    head_start = doc_start[0]
    block_count = lax.axis_size(SEQ)
    mask_last = (doc_start == last_start).astype(jnp.bfloat16)[:, None, None]
    local_state = jnp.einsum(
        "thd,the->hde", key_vecs * mask_last, value_vecs, preferred_element_type=jnp.float32
    )
    opens_before = (head_start < anchor).astype(jnp.float32)
    prefix, lows = forward_prefix(local_state, doc_start, tokens_here)
    prefix_low = (prefix * opens_before).astype(jnp.bfloat16)
    mask_first = (doc_start < anchor).astype(jnp.float32)[:, None, None]
    weights = causal_scores(queries, key_vecs, causal)
    outputs = jnp.einsum("hts,she->the", weights, value_vecs, preferred_element_type=jnp.float32)
    outputs = outputs + mask_first * jnp.einsum(
        "thd,hde->the", queries, prefix_low, preferred_element_type=jnp.float32
    )
    scaled = grad_vecs.astype(jnp.float32) * gain_rows
    totals = head_total(
        jnp.stack([jnp.sum(outputs * outputs, axis=(1, 2)), jnp.sum(scaled * outputs, axis=(1, 2))])
    )
    inv_rms = lax.rsqrt(totals[0] / WIDTH + 1e-06)
    normed = (outputs * inv_rms[:, None, None] * gain_rows).astype(jnp.bfloat16)
    grad_out = (
        inv_rms[:, None, None]
        * (scaled - outputs * (totals[1] * inv_rms * inv_rms / WIDTH)[:, None, None])
    ).astype(jnp.bfloat16)
    back_weights = causal_scores(grad_out, value_vecs, causal)
    grad_query = jnp.einsum(
        "hts,shd->thd", back_weights, key_vecs, preferred_element_type=jnp.float32
    )
    grad_query = grad_query + mask_first * jnp.einsum(
        "the,hde->thd", grad_out, prefix_low, preferred_element_type=jnp.float32
    )
    mask_head = (doc_start == head_start).astype(jnp.bfloat16)[:, None, None]
    back_state = jnp.einsum(
        "thd,the->hde", queries * mask_head, grad_out, preferred_element_type=jnp.float32
    )
    suffix, next_slab_low = backward_suffix(back_state, lows)
    place = lax.axis_index("slab")
    group = lows.shape[0]
    in_slab_next = jnp.sum(jnp.where(jnp.arange(group) == place + 1, lows, 0))
    next_low = jnp.where(place + 1 < group, in_slab_next, next_slab_low)
    continues = (next_low <= block) & (block + 1 < block_count)
    suffix = suffix * continues.astype(jnp.float32)
    suffix_low = suffix.astype(jnp.bfloat16)
    mask_tail = mask_last.astype(jnp.float32)
    grad_key = jnp.einsum("hts,thd->shd", back_weights, queries, preferred_element_type=jnp.float32)
    grad_key = grad_key + mask_tail * jnp.einsum(
        "she,hde->shd", value_vecs, suffix_low, preferred_element_type=jnp.float32
    )
    grad_value = jnp.einsum("hts,the->she", weights, grad_out, preferred_element_type=jnp.float32)
    grad_value = grad_value + mask_tail * jnp.einsum(
        "shd,hde->she", key_vecs, suffix_low, preferred_element_type=jnp.float32
    )
    flat = (tokens_here, heads_here * DH)
    return (
        normed.reshape(flat),
        grad_query.astype(jnp.bfloat16).reshape(flat),
        grad_key.astype(jnp.bfloat16).reshape(flat),
        grad_value.astype(jnp.bfloat16).reshape(flat),
    )


def solution(mesh):
    seq_count = mesh.shape["seq"]
    group = SLAB if seq_count % SLAB == 0 else 1
    slabbed = Mesh(
        mesh.devices.reshape(seq_count // group, group, mesh.shape["head"]), ("zs", "slab", "head")
    )
    rows = P(SEQ, "head")
    placed = (rows, rows, rows, rows, P("head"), P(SEQ))
    return jax.shard_map(
        on_device,
        mesh=slabbed,
        in_specs=placed,
        out_specs=(rows, rows, rows, rows),
        check_vma=False,
    )
```

```python
import jax
import jax.numpy as jnp
from jax import lax
from jax.sharding import Mesh
from jax.sharding import PartitionSpec as P

DH = 128
WIDTH = 8192
SEQ = ("zs", "slab")
SLAB = 16


def causal_scores(left_rows, right_rows, causal):
    scores = jnp.einsum("thd,shd->hts", left_rows, right_rows, preferred_element_type=jnp.float32)
    return jnp.where(causal[None], scores, 0.0).astype(jnp.bfloat16)


def weighted_sum(weights, pieces):
    return jnp.sum(weights[:, :, None, None] * pieces[None], axis=1)


def head_total(partial):
    peers = lax.axis_size("head")
    everyone = lax.all_to_all(
        jnp.broadcast_to(partial[None], (peers,) + partial.shape), "head", 0, 0, tiled=True
    )
    return jnp.sum(everyone, axis=0)


def with_rows(state, values):
    rows = jnp.zeros((state.shape[0], 8, state.shape[2]), jnp.float32)
    rows = rows.at[:, : values.shape[0], :].set(values.astype(jnp.float32)[None, :, None])
    return jnp.concatenate([state, rows], axis=1)


def forward_prefix(local_state, doc_start, tokens_here):
    slabs = lax.axis_size("zs")
    group = lax.axis_size("slab")
    slab_index = lax.axis_index("zs")
    slab_first = slab_index * group
    blocks = slab_first + jnp.arange(group, dtype=jnp.int32)
    heads, rows, lanes = local_state.shape
    width = heads * rows // group
    starts_row = jnp.zeros((group, 8, lanes), jnp.float32)
    starts_row = starts_row.at[:, 0, :].set(doc_start.astype(jnp.float32)[None, :])
    payload = jnp.concatenate([local_state.reshape(group, width, lanes), starts_row], axis=1)
    arrived = lax.all_to_all(payload, "slab", 0, 0, tiled=True)
    pieces = arrived[:, :width]
    lows = arrived[:, width, 0].astype(jnp.int32) // tokens_here
    tail_low = arrived[group - 1 :, width, lanes - 1].astype(jnp.int32) // tokens_here
    inner = (blocks[None, :] < blocks[:, None]) & (blocks[None, :] >= lows[:, None])
    in_slab = weighted_sum(inner.astype(jnp.float32), pieces)
    keep = blocks >= tail_low
    aggregate = jnp.sum(keep.astype(jnp.float32)[:, None, None] * pieces, axis=0)
    everyone = lax.all_to_all(
        jnp.broadcast_to(aggregate[None], (slabs,) + aggregate.shape), "zs", 0, 0, tiled=True
    )
    slab_ids = jnp.arange(slabs, dtype=jnp.int32)
    take = (slab_ids < slab_index) & (slab_ids >= lows[:1] // group)
    earlier = jnp.sum(take.astype(jnp.float32)[:, None, None] * everyone, axis=0)
    reaches = (lows < slab_first).astype(jnp.float32)[:, None, None]
    prefix = in_slab + reaches * earlier[None]
    prefix = lax.all_to_all(prefix, "slab", 0, 0, tiled=True).reshape(heads, rows, lanes)
    return prefix, lows


def backward_suffix(local_state, lows):
    slabs = lax.axis_size("zs")
    group = lax.axis_size("slab")
    slab_index = lax.axis_index("zs")
    slab_first = slab_index * group
    blocks = slab_first + jnp.arange(group, dtype=jnp.int32)
    heads, rows, lanes = local_state.shape
    pieces = local_state.reshape(group, heads * rows // group, lanes)
    pieces = lax.all_to_all(pieces, "slab", 0, 0, tiled=True)
    inner = (blocks[None, :] > blocks[:, None]) & (lows[None, :] <= blocks[:, None])
    in_slab = weighted_sum(inner.astype(jnp.float32), pieces)
    keep = lows < slab_first
    aggregate = jnp.sum(keep.astype(jnp.float32)[:, None, None] * pieces, axis=0)
    width = aggregate.shape[0]
    sent = with_rows(aggregate[None], lows[0:1])[0]
    everyone = lax.all_to_all(
        jnp.broadcast_to(sent[None], (slabs,) + sent.shape), "zs", 0, 0, tiled=True
    )
    slab_ids = jnp.arange(slabs, dtype=jnp.int32)
    slab_lows = everyone[:, width, 0].astype(jnp.int32)
    take = (slab_ids[None, :] > slab_index) & (slab_lows[None, :] <= blocks[:, None])
    later = weighted_sum(take.astype(jnp.float32), everyone[:, :width])
    suffix = in_slab + later
    next_slab_low = jnp.sum(jnp.where(slab_ids == slab_index + 1, slab_lows, 0))
    suffix = lax.all_to_all(suffix, "slab", 0, 0, tiled=True).reshape(heads, rows, lanes)
    return suffix, next_slab_low


def on_device(query_rows, key_rows, value_rows, grad_rows, norm_gain, doc_start):
    tokens_here = query_rows.shape[0]
    heads_here = query_rows.shape[1] // DH
    block_shape = (tokens_here, heads_here, DH)
    queries = query_rows.reshape(block_shape)
    key_vecs = key_rows.reshape(block_shape)
    value_vecs = value_rows.reshape(block_shape)
    grad_vecs = grad_rows.reshape(block_shape)
    gain_rows = norm_gain.astype(jnp.float32).reshape(heads_here, DH)
    block = lax.axis_index("zs") * lax.axis_size("slab") + lax.axis_index("slab")
    anchor = block * tokens_here
    positions = jnp.arange(tokens_here, dtype=jnp.int32)
    causal = (doc_start[:, None] == doc_start[None, :]) & (positions[None, :] <= positions[:, None])
    last_start = doc_start[-1:]
    head_start = doc_start[:1]
    block_count = lax.axis_size(SEQ)
    mask_last = (doc_start == last_start).astype(jnp.bfloat16)[:, None, None]
    local_state = jnp.einsum(
        "thd,the->hde", key_vecs * mask_last, value_vecs, preferred_element_type=jnp.float32
    )
    opens_before = (head_start < anchor).astype(jnp.float32)[:, None, None]
    prefix, lows = forward_prefix(local_state, doc_start, tokens_here)
    prefix_low = (prefix * opens_before).astype(jnp.bfloat16)
    mask_first = (doc_start < anchor).astype(jnp.float32)[:, None, None]
    weights = causal_scores(queries, key_vecs, causal)
    outputs = jnp.einsum("hts,she->the", weights, value_vecs, preferred_element_type=jnp.float32)
    outputs = outputs + mask_first * jnp.einsum(
        "thd,hde->the", queries, prefix_low, preferred_element_type=jnp.float32
    )
    scaled = grad_vecs.astype(jnp.float32) * gain_rows
    totals = head_total(
        jnp.stack([jnp.sum(outputs * outputs, axis=(1, 2)), jnp.sum(scaled * outputs, axis=(1, 2))])
    )
    inv_rms = lax.rsqrt(totals[0] / WIDTH + 1e-06)
    normed = (outputs * inv_rms[:, None, None] * gain_rows).astype(jnp.bfloat16)
    grad_out = (
        inv_rms[:, None, None]
        * (scaled - outputs * (totals[1] * inv_rms * inv_rms / WIDTH)[:, None, None])
    ).astype(jnp.bfloat16)
    back_weights = causal_scores(grad_out, value_vecs, causal)
    grad_query = jnp.einsum(
        "hts,shd->thd", back_weights, key_vecs, preferred_element_type=jnp.float32
    )
    grad_query = grad_query + mask_first * jnp.einsum(
        "the,hde->thd", grad_out, prefix_low, preferred_element_type=jnp.float32
    )
    mask_head = (doc_start == head_start).astype(jnp.bfloat16)[:, None, None]
    back_state = jnp.einsum(
        "thd,the->hde", queries * mask_head, grad_out, preferred_element_type=jnp.float32
    )
    suffix, next_slab_low = backward_suffix(back_state, lows)
    place = lax.axis_index("slab")
    group = lows.shape[0]
    in_slab_next = jnp.sum(jnp.where(jnp.arange(group) == place + 1, lows, 0))
    next_low = jnp.where(place + 1 < group, in_slab_next, next_slab_low)
    continues = (next_low <= block) & (block + 1 < block_count)
    suffix = suffix * continues.astype(jnp.float32)
    suffix_low = suffix.astype(jnp.bfloat16)
    mask_tail = mask_last.astype(jnp.float32)
    grad_key = jnp.einsum("hts,thd->shd", back_weights, queries, preferred_element_type=jnp.float32)
    grad_key = grad_key + mask_tail * jnp.einsum(
        "she,hde->shd", value_vecs, suffix_low, preferred_element_type=jnp.float32
    )
    grad_value = jnp.einsum("hts,the->she", weights, grad_out, preferred_element_type=jnp.float32)
    grad_value = grad_value + mask_tail * jnp.einsum(
        "shd,hde->she", key_vecs, suffix_low, preferred_element_type=jnp.float32
    )
    flat = (tokens_here, heads_here * DH)
    return (
        normed.reshape(flat),
        grad_query.astype(jnp.bfloat16).reshape(flat),
        grad_key.astype(jnp.bfloat16).reshape(flat),
        grad_value.astype(jnp.bfloat16).reshape(flat),
    )


def solution(mesh):
    seq_count = mesh.shape["seq"]
    group = SLAB if seq_count % SLAB == 0 else 1
    slabbed = Mesh(
        mesh.devices.reshape(seq_count // group, group, mesh.shape["head"]), ("zs", "slab", "head")
    )
    rows = P(SEQ, "head")
    placed = (rows, rows, rows, rows, P("head"), P(SEQ))
    return jax.shard_map(
        on_device,
        mesh=slabbed,
        in_specs=placed,
        out_specs=(rows, rows, rows, rows),
        check_vma=False,
    )
```

```python
import jax
import jax.numpy as jnp
from jax import lax
from jax.sharding import Mesh
from jax.sharding import PartitionSpec as P

DH = 128
WIDTH = 8192
SEQ = ("zs", "slab")
SLAB = 16


def causal_scores(left_rows, right_rows, causal):
    scores = jnp.einsum("thd,shd->hts", left_rows, right_rows, preferred_element_type=jnp.float32)
    return jnp.where(causal[None], scores, 0.0).astype(jnp.bfloat16)


def weighted_sum(weights, pieces):
    return jnp.sum(weights[:, :, None, None] * pieces[None], axis=1)


def head_total(partial):
    peers = lax.axis_size("head")
    everyone = lax.all_to_all(
        jnp.broadcast_to(partial[None], (peers,) + partial.shape), "head", 0, 0, tiled=True
    )
    return jnp.sum(everyone, axis=0)


def with_rows(state, values):
    rows = jnp.zeros((state.shape[0], 8, state.shape[2]), jnp.float32)
    rows = rows.at[:, : values.shape[0], :].set(values.astype(jnp.float32)[None, :, None])
    return jnp.concatenate([state, rows], axis=1)


def forward_prefix(local_state, doc_start, tokens_here):
    slabs = lax.axis_size("zs")
    group = lax.axis_size("slab")
    slab_index = lax.axis_index("zs")
    slab_first = slab_index * group
    blocks = slab_first + jnp.arange(group, dtype=jnp.int32)
    heads, rows, lanes = local_state.shape
    width = heads * rows // group
    starts_row = jnp.zeros((group, 8, lanes), jnp.float32)
    starts_row = starts_row.at[:, 0, :].set(doc_start.astype(jnp.float32)[None, :])
    payload = jnp.concatenate([local_state.reshape(group, width, lanes), starts_row], axis=1)
    arrived = lax.all_to_all(payload, "slab", 0, 0, tiled=True)
    pieces = arrived[:, :width]
    lows = arrived[:, width, 0].astype(jnp.int32) // tokens_here
    tail_low = arrived[group - 1 :, width, lanes - 1].astype(jnp.int32) // tokens_here
    inner = (blocks[None, :] < blocks[:, None]) & (blocks[None, :] >= lows[:, None])
    in_slab = weighted_sum(inner.astype(jnp.float32), pieces)
    keep = blocks >= tail_low
    aggregate = jnp.sum(keep.astype(jnp.float32)[:, None, None] * pieces, axis=0)
    everyone = lax.all_to_all(
        jnp.broadcast_to(aggregate[None], (slabs,) + aggregate.shape), "zs", 0, 0, tiled=True
    )
    slab_ids = jnp.arange(slabs, dtype=jnp.int32)
    take = (slab_ids < slab_index) & (slab_ids >= lows[:1] // group)
    earlier = jnp.sum(take.astype(jnp.float32)[:, None, None] * everyone, axis=0)
    reaches = (lows < slab_first).astype(jnp.float32)[:, None, None]
    prefix = in_slab + reaches * earlier[None]
    prefix = lax.all_to_all(prefix, "slab", 0, 0, tiled=True).reshape(heads, rows, lanes)
    return prefix, lows


def backward_suffix(local_state, lows):
    slabs = lax.axis_size("zs")
    group = lax.axis_size("slab")
    slab_index = lax.axis_index("zs")
    slab_first = slab_index * group
    blocks = slab_first + jnp.arange(group, dtype=jnp.int32)
    heads, rows, lanes = local_state.shape
    pieces = local_state.reshape(group, heads * rows // group, lanes)
    pieces = lax.all_to_all(pieces, "slab", 0, 0, tiled=True)
    inner = (blocks[None, :] > blocks[:, None]) & (lows[None, :] <= blocks[:, None])
    in_slab = weighted_sum(inner.astype(jnp.float32), pieces)
    keep = lows < slab_first
    aggregate = jnp.sum(keep.astype(jnp.float32)[:, None, None] * pieces, axis=0)
    width = aggregate.shape[0]
    sent = with_rows(aggregate[None], lows[0:1])[0]
    everyone = lax.all_to_all(
        jnp.broadcast_to(sent[None], (slabs,) + sent.shape), "zs", 0, 0, tiled=True
    )
    slab_ids = jnp.arange(slabs, dtype=jnp.int32)
    slab_lows = everyone[:, width, 0].astype(jnp.int32)
    take = (slab_ids[None, :] > slab_index) & (slab_lows[None, :] <= blocks[:, None])
    later = weighted_sum(take.astype(jnp.float32), everyone[:, :width])
    suffix = in_slab + later
    next_slab_low = jnp.sum(jnp.where(slab_ids == slab_index + 1, slab_lows, 0))
    suffix = lax.all_to_all(suffix, "slab", 0, 0, tiled=True).reshape(heads, rows, lanes)
    return suffix, next_slab_low


def on_device(query_rows, key_rows, value_rows, grad_rows, norm_gain, doc_start):
    tokens_here = query_rows.shape[0]
    heads_here = query_rows.shape[1] // DH
    block_shape = (tokens_here, heads_here, DH)
    queries = query_rows.reshape(block_shape)
    key_vecs = key_rows.reshape(block_shape)
    value_vecs = value_rows.reshape(block_shape)
    grad_vecs = grad_rows.reshape(block_shape)
    gain_rows = norm_gain.astype(jnp.float32).reshape(heads_here, DH)
    block = lax.axis_index("zs") * lax.axis_size("slab") + lax.axis_index("slab")
    anchor = block * tokens_here
    positions = jnp.arange(tokens_here, dtype=jnp.int32)
    causal = (doc_start[:, None] == doc_start[None, :]) & (positions[None, :] <= positions[:, None])
    last_start = jnp.max(doc_start, keepdims=True)
    head_start = jnp.min(doc_start, keepdims=True)
    block_count = lax.axis_size(SEQ)
    mask_last = (doc_start == last_start).astype(jnp.bfloat16)[:, None, None]
    local_state = jnp.einsum(
        "thd,the->hde", key_vecs * mask_last, value_vecs, preferred_element_type=jnp.float32
    )
    opens_before = (head_start < anchor).astype(jnp.float32)[:, None, None]
    prefix, lows = forward_prefix(local_state, doc_start, tokens_here)
    prefix_low = (prefix * opens_before).astype(jnp.bfloat16)
    mask_first = (doc_start < anchor).astype(jnp.float32)[:, None, None]
    weights = causal_scores(queries, key_vecs, causal)
    outputs = jnp.einsum("hts,she->the", weights, value_vecs, preferred_element_type=jnp.float32)
    outputs = outputs + mask_first * jnp.einsum(
        "thd,hde->the", queries, prefix_low, preferred_element_type=jnp.float32
    )
    scaled = grad_vecs.astype(jnp.float32) * gain_rows
    totals = head_total(
        jnp.stack([jnp.sum(outputs * outputs, axis=(1, 2)), jnp.sum(scaled * outputs, axis=(1, 2))])
    )
    inv_rms = lax.rsqrt(totals[0] / WIDTH + 1e-06)
    normed = (outputs * inv_rms[:, None, None] * gain_rows).astype(jnp.bfloat16)
    grad_out = (
        inv_rms[:, None, None]
        * (scaled - outputs * (totals[1] * inv_rms * inv_rms / WIDTH)[:, None, None])
    ).astype(jnp.bfloat16)
    back_weights = causal_scores(grad_out, value_vecs, causal)
    grad_query = jnp.einsum(
        "hts,shd->thd", back_weights, key_vecs, preferred_element_type=jnp.float32
    )
    grad_query = grad_query + mask_first * jnp.einsum(
        "the,hde->thd", grad_out, prefix_low, preferred_element_type=jnp.float32
    )
    mask_head = (doc_start == head_start).astype(jnp.bfloat16)[:, None, None]
    back_state = jnp.einsum(
        "thd,the->hde", queries * mask_head, grad_out, preferred_element_type=jnp.float32
    )
    suffix, next_slab_low = backward_suffix(back_state, lows)
    place = lax.axis_index("slab")
    group = lows.shape[0]
    in_slab_next = jnp.sum(jnp.where(jnp.arange(group) == place + 1, lows, 0))
    next_low = jnp.where(place + 1 < group, in_slab_next, next_slab_low)
    continues = (next_low <= block) & (block + 1 < block_count)
    suffix = suffix * continues.astype(jnp.float32)
    suffix_low = suffix.astype(jnp.bfloat16)
    mask_tail = mask_last.astype(jnp.float32)
    grad_key = jnp.einsum("hts,thd->shd", back_weights, queries, preferred_element_type=jnp.float32)
    grad_key = grad_key + mask_tail * jnp.einsum(
        "she,hde->shd", value_vecs, suffix_low, preferred_element_type=jnp.float32
    )
    grad_value = jnp.einsum("hts,the->she", weights, grad_out, preferred_element_type=jnp.float32)
    grad_value = grad_value + mask_tail * jnp.einsum(
        "shd,hde->she", key_vecs, suffix_low, preferred_element_type=jnp.float32
    )
    flat = (tokens_here, heads_here * DH)
    return (
        normed.reshape(flat),
        grad_query.astype(jnp.bfloat16).reshape(flat),
        grad_key.astype(jnp.bfloat16).reshape(flat),
        grad_value.astype(jnp.bfloat16).reshape(flat),
    )


def solution(mesh):
    seq_count = mesh.shape["seq"]
    group = SLAB if seq_count % SLAB == 0 else 1
    slabbed = Mesh(
        mesh.devices.reshape(seq_count // group, group, mesh.shape["head"]), ("zs", "slab", "head")
    )
    rows = P(SEQ, "head")
    placed = (rows, rows, rows, rows, P("head"), P(SEQ))
    return jax.shard_map(
        on_device,
        mesh=slabbed,
        in_specs=placed,
        out_specs=(rows, rows, rows, rows),
        check_vma=False,
    )
```

```python
import jax
import jax.numpy as jnp
from jax import lax
from jax.sharding import Mesh
from jax.sharding import PartitionSpec as P

DH = 128
WIDTH = 8192
SEQ = ("zs", "slab")
SLAB = 16


def causal_scores(left_rows, right_rows, causal):
    scores = jnp.einsum("thd,shd->hts", left_rows, right_rows, preferred_element_type=jnp.float32)
    return jnp.where(causal[None], scores, 0.0).astype(jnp.bfloat16)


def weighted_sum(weights, pieces):
    return jnp.sum(weights[:, :, None, None] * pieces[None], axis=1)


def head_total(partial):
    peers = lax.axis_size("head")
    everyone = lax.all_to_all(
        jnp.broadcast_to(partial[None], (peers,) + partial.shape), "head", 0, 0, tiled=True
    )
    return jnp.sum(everyone, axis=0)


def with_rows(state, values):
    rows = jnp.zeros((state.shape[0], 8, state.shape[2]), jnp.float32)
    rows = rows.at[:, : values.shape[0], :].set(values.astype(jnp.float32)[None, :, None])
    return jnp.concatenate([state, rows], axis=1)


def forward_prefix(local_state, doc_start, tokens_here):
    slabs = lax.axis_size("zs")
    group = lax.axis_size("slab")
    slab_index = lax.axis_index("zs")
    slab_first = slab_index * group
    blocks = slab_first + jnp.arange(group, dtype=jnp.int32)
    heads, rows, lanes = local_state.shape
    width = heads * rows // group
    starts_row = jnp.zeros((group, 8, lanes), jnp.float32)
    starts_row = starts_row.at[:, 0, :].set(doc_start.astype(jnp.float32)[None, :])
    payload = jnp.concatenate([local_state.reshape(group, width, lanes), starts_row], axis=1)
    arrived = lax.all_to_all(payload, "slab", 0, 0, tiled=True)
    pieces = arrived[:, :width]
    lows = arrived[:, width, 0].astype(jnp.int32) // tokens_here
    tail_low = arrived[group - 1 :, width, lanes - 1].astype(jnp.int32) // tokens_here
    inner = (blocks[None, :] < blocks[:, None]) & (blocks[None, :] >= lows[:, None])
    in_slab = weighted_sum(inner.astype(jnp.float32), pieces)
    keep = blocks >= tail_low
    aggregate = jnp.sum(keep.astype(jnp.float32)[:, None, None] * pieces, axis=0)
    everyone = lax.all_to_all(
        jnp.broadcast_to(aggregate[None], (slabs,) + aggregate.shape), "zs", 0, 0, tiled=True
    )
    slab_ids = jnp.arange(slabs, dtype=jnp.int32)
    take = (slab_ids < slab_index) & (slab_ids >= lows[:1] // group)
    earlier = jnp.sum(take.astype(jnp.float32)[:, None, None] * everyone, axis=0)
    reaches = (lows < slab_first).astype(jnp.float32)[:, None, None]
    prefix = in_slab + reaches * earlier[None]
    prefix = lax.all_to_all(prefix, "slab", 0, 0, tiled=True).reshape(heads, rows, lanes)
    return prefix, lows


def backward_suffix(local_state, lows):
    slabs = lax.axis_size("zs")
    group = lax.axis_size("slab")
    slab_index = lax.axis_index("zs")
    slab_first = slab_index * group
    blocks = slab_first + jnp.arange(group, dtype=jnp.int32)
    heads, rows, lanes = local_state.shape
    pieces = local_state.reshape(group, heads * rows // group, lanes)
    pieces = lax.all_to_all(pieces, "slab", 0, 0, tiled=True)
    inner = (blocks[None, :] > blocks[:, None]) & (lows[None, :] <= blocks[:, None])
    in_slab = weighted_sum(inner.astype(jnp.float32), pieces)
    keep = lows < slab_first
    aggregate = jnp.sum(keep.astype(jnp.float32)[:, None, None] * pieces, axis=0)
    width = aggregate.shape[0]
    sent = with_rows(aggregate[None], lows[0:1])[0]
    everyone = lax.all_to_all(
        jnp.broadcast_to(sent[None], (slabs,) + sent.shape), "zs", 0, 0, tiled=True
    )
    slab_ids = jnp.arange(slabs, dtype=jnp.int32)
    slab_lows = everyone[:, width, 0].astype(jnp.int32)
    take = (slab_ids[None, :] > slab_index) & (slab_lows[None, :] <= blocks[:, None])
    later = weighted_sum(take.astype(jnp.float32), everyone[:, :width])
    suffix = in_slab + later
    next_slab_low = jnp.sum(jnp.where(slab_ids == slab_index + 1, slab_lows, 0))
    suffix = lax.all_to_all(suffix, "slab", 0, 0, tiled=True).reshape(heads, rows, lanes)
    return suffix, next_slab_low


def on_device(query_rows, key_rows, value_rows, grad_rows, norm_gain, doc_start):
    tokens_here = query_rows.shape[0]
    heads_here = query_rows.shape[1] // DH
    block_shape = (tokens_here, heads_here, DH)
    queries = query_rows.reshape(block_shape)
    key_vecs = key_rows.reshape(block_shape)
    value_vecs = value_rows.reshape(block_shape)
    grad_vecs = grad_rows.reshape(block_shape)
    gain_rows = norm_gain.astype(jnp.float32).reshape(heads_here, DH)
    block = lax.axis_index("zs") * lax.axis_size("slab") + lax.axis_index("slab")
    anchor = block * tokens_here
    positions = jnp.arange(tokens_here, dtype=jnp.int32)
    causal = (doc_start[:, None] == doc_start[None, :]) & (positions[None, :] <= positions[:, None])
    last_start = jnp.max(doc_start, keepdims=True)
    head_start = jnp.min(doc_start, keepdims=True)
    block_count = lax.axis_size(SEQ)
    mask_last = (doc_start == last_start).astype(jnp.bfloat16)[:, None, None]
    local_state = jnp.einsum(
        "thd,the->hde", key_vecs * mask_last, value_vecs, preferred_element_type=jnp.float32
    )
    opens_before = (head_start < anchor).astype(jnp.float32)[:, None, None]
    prefix, lows = forward_prefix(local_state, doc_start, tokens_here)
    prefix_low = (prefix * opens_before).astype(jnp.bfloat16)
    mask_first = (doc_start < anchor).astype(jnp.float32)[:, None, None]
    weights = causal_scores(queries, key_vecs, causal)
    outputs = jnp.einsum("hts,she->the", weights, value_vecs, preferred_element_type=jnp.float32)
    outputs = outputs + mask_first * jnp.einsum(
        "thd,hde->the", queries, prefix_low, preferred_element_type=jnp.float32
    )
    scaled = grad_vecs.astype(jnp.float32) * gain_rows
    totals = head_total(
        jnp.stack([jnp.sum(outputs * outputs, axis=(1, 2)), jnp.sum(scaled * outputs, axis=(1, 2))])
    )
    inv_rms = lax.rsqrt(totals[0] / WIDTH + 1e-06)
    normed = (outputs * inv_rms[:, None, None] * gain_rows).astype(jnp.bfloat16)
    grad_out = (
        inv_rms[:, None, None]
        * (scaled - outputs * (totals[1] * inv_rms * inv_rms / WIDTH)[:, None, None])
    ).astype(jnp.bfloat16)
    back_weights = causal_scores(grad_out, value_vecs, causal)
    grad_query = jnp.einsum(
        "hts,shd->thd", back_weights, key_vecs, preferred_element_type=jnp.float32
    )
    grad_query = grad_query + mask_first * jnp.einsum(
        "the,hde->thd", grad_out, prefix_low, preferred_element_type=jnp.float32
    )
    mask_head = (doc_start == head_start).astype(jnp.bfloat16)[:, None, None]
    back_state = jnp.einsum(
        "thd,the->hde", queries * mask_head, grad_out, preferred_element_type=jnp.float32
    )
    suffix, next_slab_low = backward_suffix(back_state, lows)
    place = lax.axis_index("slab")
    group = lows.shape[0]
    in_slab_next = jnp.sum(jnp.where(jnp.arange(group) == place + 1, lows, 0))
    next_low = jnp.where(place + 1 < group, in_slab_next, next_slab_low)
    continues = (next_low <= block) & (block + 1 < block_count)
    suffix = suffix * continues.astype(jnp.float32)
    suffix_low = suffix.astype(jnp.bfloat16)
    mask_tail = mask_last.astype(jnp.float32)[:, :, 0]
    flat = (tokens_here, heads_here * DH)
    diagonal = jnp.eye(heads_here, dtype=jnp.bfloat16)[:, None, :, None]
    spread_value = (diagonal * suffix_low[:, :, None, :]).reshape(flat[1], flat[1])
    spread_key = (diagonal * jnp.swapaxes(suffix_low, 1, 2)[:, :, None, :]).reshape(flat[1], flat[1])
    grad_key = jnp.einsum("hts,thd->shd", back_weights, queries, preferred_element_type=jnp.float32)
    grad_key = grad_key.reshape(flat) + mask_tail * jnp.dot(
        value_rows, spread_key, preferred_element_type=jnp.float32
    )
    grad_value = jnp.einsum("hts,the->she", weights, grad_out, preferred_element_type=jnp.float32)
    grad_value = grad_value.reshape(flat) + mask_tail * jnp.dot(
        key_rows, spread_value, preferred_element_type=jnp.float32
    )
    return (
        normed.reshape(flat),
        grad_query.astype(jnp.bfloat16).reshape(flat),
        grad_key.astype(jnp.bfloat16),
        grad_value.astype(jnp.bfloat16),
    )


def solution(mesh):
    seq_count = mesh.shape["seq"]
    group = SLAB if seq_count % SLAB == 0 else 1
    slabbed = Mesh(
        mesh.devices.reshape(seq_count // group, group, mesh.shape["head"]), ("zs", "slab", "head")
    )
    rows = P(SEQ, "head")
    placed = (rows, rows, rows, rows, P("head"), P(SEQ))
    return jax.shard_map(
        on_device,
        mesh=slabbed,
        in_specs=placed,
        out_specs=(rows, rows, rows, rows),
        check_vma=False,
    )
```

```python
import jax
import jax.numpy as jnp
from jax import lax
from jax.sharding import Mesh
from jax.sharding import PartitionSpec as P

DH = 128
WIDTH = 8192
SEQ = ("zs", "slab")
SLAB = 16


def causal_scores(left_rows, right_rows, causal):
    scores = jnp.einsum("thd,shd->hts", left_rows, right_rows, preferred_element_type=jnp.float32)
    return jnp.where(causal[None], scores, 0.0).astype(jnp.bfloat16)


def weighted_sum(weights, pieces):
    return jnp.sum(weights[:, :, None, None] * pieces[None], axis=1)


def head_total(partial):
    peers = lax.axis_size("head")
    everyone = lax.all_to_all(
        jnp.broadcast_to(partial[None], (peers,) + partial.shape), "head", 0, 0, tiled=True
    )
    return jnp.sum(everyone, axis=0)


def with_rows(state, values):
    rows = jnp.zeros((state.shape[0], 8, state.shape[2]), jnp.float32)
    rows = rows.at[:, : values.shape[0], :].set(values.astype(jnp.float32)[None, :, None])
    return jnp.concatenate([state, rows], axis=1)


def forward_prefix(local_state, doc_start, tokens_here):
    slabs = lax.axis_size("zs")
    group = lax.axis_size("slab")
    slab_index = lax.axis_index("zs")
    slab_first = slab_index * group
    blocks = slab_first + jnp.arange(group, dtype=jnp.int32)
    heads, rows, lanes = local_state.shape
    width = heads * rows // group
    starts_row = jnp.zeros((group, 8, lanes), jnp.float32)
    starts_row = starts_row.at[:, 0, :].set(doc_start.astype(jnp.float32)[None, :])
    payload = jnp.concatenate([local_state.reshape(group, width, lanes), starts_row], axis=1)
    arrived = lax.all_to_all(payload, "slab", 0, 0, tiled=True)
    pieces = arrived[:, :width]
    lows = arrived[:, width, 0].astype(jnp.int32) // tokens_here
    tail_low = arrived[group - 1 :, width, lanes - 1].astype(jnp.int32) // tokens_here
    inner = (blocks[None, :] < blocks[:, None]) & (blocks[None, :] >= lows[:, None])
    in_slab = weighted_sum(inner.astype(jnp.float32), pieces)
    keep = jnp.broadcast_to((blocks >= tail_low).astype(jnp.float32)[None, :], (slabs, group))
    everyone = lax.all_to_all(weighted_sum(keep, pieces), "zs", 0, 0, tiled=True)
    slab_ids = jnp.arange(slabs, dtype=jnp.int32)
    take = (slab_ids < slab_index) & (slab_ids >= lows[:1] // group)
    earlier = jnp.sum(take.astype(jnp.float32)[:, None, None] * everyone, axis=0)
    reaches = (lows < slab_first).astype(jnp.float32)[:, None, None]
    prefix = in_slab + reaches * earlier[None]
    prefix = lax.all_to_all(prefix, "slab", 0, 0, tiled=True).reshape(heads, rows, lanes)
    return prefix, lows


def backward_suffix(local_state, lows):
    slabs = lax.axis_size("zs")
    group = lax.axis_size("slab")
    slab_index = lax.axis_index("zs")
    slab_first = slab_index * group
    blocks = slab_first + jnp.arange(group, dtype=jnp.int32)
    heads, rows, lanes = local_state.shape
    pieces = local_state.reshape(group, heads * rows // group, lanes)
    pieces = lax.all_to_all(pieces, "slab", 0, 0, tiled=True)
    inner = (blocks[None, :] > blocks[:, None]) & (lows[None, :] <= blocks[:, None])
    in_slab = weighted_sum(inner.astype(jnp.float32), pieces)
    keep = jnp.broadcast_to((lows < slab_first).astype(jnp.float32)[None, :], (slabs, group))
    width = pieces.shape[1]
    sent = with_rows(weighted_sum(keep, pieces), lows[0:1])
    everyone = lax.all_to_all(sent, "zs", 0, 0, tiled=True)
    slab_ids = jnp.arange(slabs, dtype=jnp.int32)
    slab_lows = everyone[:, width, 0].astype(jnp.int32)
    take = (slab_ids[None, :] > slab_index) & (slab_lows[None, :] <= blocks[:, None])
    later = weighted_sum(take.astype(jnp.float32), everyone[:, :width])
    suffix = in_slab + later
    next_slab_low = jnp.sum(jnp.where(slab_ids == slab_index + 1, slab_lows, 0))
    suffix = lax.all_to_all(suffix, "slab", 0, 0, tiled=True).reshape(heads, rows, lanes)
    return suffix, next_slab_low


def on_device(query_rows, key_rows, value_rows, grad_rows, norm_gain, doc_start):
    tokens_here = query_rows.shape[0]
    heads_here = query_rows.shape[1] // DH
    block_shape = (tokens_here, heads_here, DH)
    queries = query_rows.reshape(block_shape)
    key_vecs = key_rows.reshape(block_shape)
    value_vecs = value_rows.reshape(block_shape)
    grad_vecs = grad_rows.reshape(block_shape)
    gain_rows = norm_gain.astype(jnp.float32).reshape(heads_here, DH)
    block = lax.axis_index("zs") * lax.axis_size("slab") + lax.axis_index("slab")
    anchor = block * tokens_here
    positions = jnp.arange(tokens_here, dtype=jnp.int32)
    causal = (doc_start[:, None] == doc_start[None, :]) & (positions[None, :] <= positions[:, None])
    last_start = jnp.max(doc_start, keepdims=True)
    head_start = jnp.min(doc_start, keepdims=True)
    block_count = lax.axis_size(SEQ)
    mask_last = (doc_start == last_start).astype(jnp.bfloat16)[:, None, None]
    local_state = jnp.einsum(
        "thd,the->hde", key_vecs * mask_last, value_vecs, preferred_element_type=jnp.float32
    )
    opens_before = (head_start < anchor).astype(jnp.float32)[:, None, None]
    prefix, lows = forward_prefix(local_state, doc_start, tokens_here)
    prefix_low = (prefix * opens_before).astype(jnp.bfloat16)
    mask_first = (doc_start < anchor).astype(jnp.float32)[:, None, None]
    weights = causal_scores(queries, key_vecs, causal)
    outputs = jnp.einsum("hts,she->the", weights, value_vecs, preferred_element_type=jnp.float32)
    outputs = outputs + mask_first * jnp.einsum(
        "thd,hde->the", queries, prefix_low, preferred_element_type=jnp.float32
    )
    scaled = grad_vecs.astype(jnp.float32) * gain_rows
    totals = head_total(
        jnp.stack([jnp.sum(outputs * outputs, axis=(1, 2)), jnp.sum(scaled * outputs, axis=(1, 2))])
    )
    inv_rms = lax.rsqrt(totals[0] / WIDTH + 1e-06)
    normed = (outputs * inv_rms[:, None, None] * gain_rows).astype(jnp.bfloat16)
    grad_out = (
        inv_rms[:, None, None]
        * (scaled - outputs * (totals[1] * inv_rms * inv_rms / WIDTH)[:, None, None])
    ).astype(jnp.bfloat16)
    back_weights = causal_scores(grad_out, value_vecs, causal)
    grad_query = jnp.einsum(
        "hts,shd->thd", back_weights, key_vecs, preferred_element_type=jnp.float32
    )
    grad_query = grad_query + mask_first * jnp.einsum(
        "the,hde->thd", grad_out, prefix_low, preferred_element_type=jnp.float32
    )
    mask_head = (doc_start == head_start).astype(jnp.bfloat16)[:, None, None]
    back_state = jnp.einsum(
        "thd,the->hde", queries * mask_head, grad_out, preferred_element_type=jnp.float32
    )
    suffix, next_slab_low = backward_suffix(back_state, lows)
    place = lax.axis_index("slab")
    group = lows.shape[0]
    in_slab_next = jnp.sum(jnp.where(jnp.arange(group) == place + 1, lows, 0))
    next_low = jnp.where(place + 1 < group, in_slab_next, next_slab_low)
    continues = (next_low <= block) & (block + 1 < block_count)
    suffix = suffix * continues.astype(jnp.float32)
    suffix_low = suffix.astype(jnp.bfloat16)
    mask_tail = mask_last.astype(jnp.float32)
    grad_key = jnp.einsum("hts,thd->shd", back_weights, queries, preferred_element_type=jnp.float32)
    grad_key = grad_key + mask_tail * jnp.einsum(
        "she,hde->shd", value_vecs, suffix_low, preferred_element_type=jnp.float32
    )
    grad_value = jnp.einsum("hts,the->she", weights, grad_out, preferred_element_type=jnp.float32)
    grad_value = grad_value + mask_tail * jnp.einsum(
        "shd,hde->she", key_vecs, suffix_low, preferred_element_type=jnp.float32
    )
    flat = (tokens_here, heads_here * DH)
    return (
        normed.reshape(flat),
        grad_query.astype(jnp.bfloat16).reshape(flat),
        grad_key.astype(jnp.bfloat16).reshape(flat),
        grad_value.astype(jnp.bfloat16).reshape(flat),
    )


def solution(mesh):
    seq_count = mesh.shape["seq"]
    group = SLAB if seq_count % SLAB == 0 else 1
    slabbed = Mesh(
        mesh.devices.reshape(seq_count // group, group, mesh.shape["head"]), ("zs", "slab", "head")
    )
    rows = P(SEQ, "head")
    placed = (rows, rows, rows, rows, P("head"), P(SEQ))
    return jax.shard_map(
        on_device,
        mesh=slabbed,
        in_specs=placed,
        out_specs=(rows, rows, rows, rows),
        check_vma=False,
    )
```

```python
import jax
import jax.numpy as jnp
from jax import lax
from jax.sharding import Mesh
from jax.sharding import PartitionSpec as P

DH = 128
WIDTH = 8192
SEQ = ("zs", "slab")
SLAB = 16


def causal_scores(left_rows, right_rows, causal):
    scores = jnp.einsum("thd,shd->hts", left_rows, right_rows, preferred_element_type=jnp.float32)
    return jnp.where(causal[None], scores, 0.0).astype(jnp.bfloat16)


def weighted_sum(weights, pieces):
    return jnp.sum(weights[:, :, None, None] * pieces[None], axis=1)


def head_total(partial):
    peers = lax.axis_size("head")
    everyone = lax.all_to_all(
        jnp.broadcast_to(partial[None], (peers,) + partial.shape), "head", 0, 0, tiled=True
    )
    return jnp.sum(everyone, axis=0)


def with_rows(state, values):
    rows = jnp.zeros((state.shape[0], 8, state.shape[2]), jnp.float32)
    rows = rows.at[:, : values.shape[0], :].set(values.astype(jnp.float32)[None, :, None])
    return jnp.concatenate([state, rows], axis=1)


def forward_prefix(local_state, doc_start, tokens_here):
    slabs = lax.axis_size("zs")
    group = lax.axis_size("slab")
    slab_index = lax.axis_index("zs")
    slab_first = slab_index * group
    blocks = slab_first + jnp.arange(group, dtype=jnp.int32)
    group_heads, padded, lanes = local_state.shape
    width = padded - 8
    heads, rows = group_heads * width // DH, DH
    starts_row = jnp.zeros((group, width + 8, lanes), jnp.float32)
    starts_row = starts_row.at[:, width, :].set(doc_start.astype(jnp.float32)[None, :])
    payload = local_state + starts_row
    arrived = lax.all_to_all(payload, "slab", 0, 0, tiled=True)
    pieces = arrived[:, :width]
    lows = arrived[:, width, 0].astype(jnp.int32) // tokens_here
    tail_low = arrived[group - 1 :, width, lanes - 1].astype(jnp.int32) // tokens_here
    inner = (blocks[None, :] < blocks[:, None]) & (blocks[None, :] >= lows[:, None])
    in_slab = weighted_sum(inner.astype(jnp.float32), pieces)
    keep = jnp.broadcast_to((blocks >= tail_low).astype(jnp.float32)[None, :], (slabs, group))
    everyone = lax.all_to_all(weighted_sum(keep, pieces), "zs", 0, 0, tiled=True)
    slab_ids = jnp.arange(slabs, dtype=jnp.int32)
    take = (slab_ids < slab_index) & (slab_ids >= lows[:1] // group)
    earlier = jnp.sum(take.astype(jnp.float32)[:, None, None] * everyone, axis=0)
    reaches = (lows < slab_first).astype(jnp.float32)[:, None, None]
    prefix = in_slab + reaches * earlier[None]
    prefix = lax.all_to_all(prefix, "slab", 0, 0, tiled=True).reshape(heads, rows, lanes)
    return prefix, lows


def backward_suffix(local_state, lows):
    slabs = lax.axis_size("zs")
    group = lax.axis_size("slab")
    slab_index = lax.axis_index("zs")
    slab_first = slab_index * group
    blocks = slab_first + jnp.arange(group, dtype=jnp.int32)
    heads, rows, lanes = local_state.shape
    pieces = local_state.reshape(group, heads * rows // group, lanes)
    pieces = lax.all_to_all(pieces, "slab", 0, 0, tiled=True)
    inner = (blocks[None, :] > blocks[:, None]) & (lows[None, :] <= blocks[:, None])
    in_slab = weighted_sum(inner.astype(jnp.float32), pieces)
    keep = jnp.broadcast_to((lows < slab_first).astype(jnp.float32)[None, :], (slabs, group))
    width = pieces.shape[1]
    sent = with_rows(weighted_sum(keep, pieces), lows[0:1])
    everyone = lax.all_to_all(sent, "zs", 0, 0, tiled=True)
    slab_ids = jnp.arange(slabs, dtype=jnp.int32)
    slab_lows = everyone[:, width, 0].astype(jnp.int32)
    take = (slab_ids[None, :] > slab_index) & (slab_lows[None, :] <= blocks[:, None])
    later = weighted_sum(take.astype(jnp.float32), everyone[:, :width])
    suffix = in_slab + later
    next_slab_low = jnp.sum(jnp.where(slab_ids == slab_index + 1, slab_lows, 0))
    suffix = lax.all_to_all(suffix, "slab", 0, 0, tiled=True).reshape(heads, rows, lanes)
    return suffix, next_slab_low


def on_device(query_rows, key_rows, value_rows, grad_rows, norm_gain, doc_start):
    tokens_here = query_rows.shape[0]
    heads_here = query_rows.shape[1] // DH
    block_shape = (tokens_here, heads_here, DH)
    queries = query_rows.reshape(block_shape)
    key_vecs = key_rows.reshape(block_shape)
    value_vecs = value_rows.reshape(block_shape)
    grad_vecs = grad_rows.reshape(block_shape)
    gain_rows = norm_gain.astype(jnp.float32).reshape(heads_here, DH)
    block = lax.axis_index("zs") * lax.axis_size("slab") + lax.axis_index("slab")
    anchor = block * tokens_here
    positions = jnp.arange(tokens_here, dtype=jnp.int32)
    causal = (doc_start[:, None] == doc_start[None, :]) & (positions[None, :] <= positions[:, None])
    last_start = jnp.max(doc_start, keepdims=True)
    head_start = jnp.min(doc_start, keepdims=True)
    block_count = lax.axis_size(SEQ)
    mask_last = (doc_start == last_start).astype(jnp.bfloat16)[:, None, None]
    halves = SLAB // heads_here
    split_keys = (key_vecs * mask_last).reshape(tokens_here, heads_here, halves, DH // halves)
    split_keys = jnp.pad(split_keys, ((0, 0), (0, 0), (0, 0), (0, 8)))
    local_state = jnp.einsum(
        "thcd,the->hcde", split_keys, value_vecs, preferred_element_type=jnp.float32
    ).reshape(heads_here * halves, DH // halves + 8, DH)
    opens_before = (head_start < anchor).astype(jnp.float32)[:, None, None]
    prefix, lows = forward_prefix(local_state, doc_start, tokens_here)
    prefix_low = (prefix * opens_before).astype(jnp.bfloat16)
    mask_first = (doc_start < anchor).astype(jnp.float32)[:, None, None]
    weights = causal_scores(queries, key_vecs, causal)
    outputs = jnp.einsum("hts,she->the", weights, value_vecs, preferred_element_type=jnp.float32)
    outputs = outputs + mask_first * jnp.einsum(
        "thd,hde->the", queries, prefix_low, preferred_element_type=jnp.float32
    )
    scaled = grad_vecs.astype(jnp.float32) * gain_rows
    totals = head_total(
        jnp.stack([jnp.sum(outputs * outputs, axis=(1, 2)), jnp.sum(scaled * outputs, axis=(1, 2))])
    )
    inv_rms = lax.rsqrt(totals[0] / WIDTH + 1e-06)
    normed = (outputs * inv_rms[:, None, None] * gain_rows).astype(jnp.bfloat16)
    grad_out = (
        inv_rms[:, None, None]
        * (scaled - outputs * (totals[1] * inv_rms * inv_rms / WIDTH)[:, None, None])
    ).astype(jnp.bfloat16)
    back_weights = causal_scores(grad_out, value_vecs, causal)
    grad_query = jnp.einsum(
        "hts,shd->thd", back_weights, key_vecs, preferred_element_type=jnp.float32
    )
    grad_query = grad_query + mask_first * jnp.einsum(
        "the,hde->thd", grad_out, prefix_low, preferred_element_type=jnp.float32
    )
    mask_head = (doc_start == head_start).astype(jnp.bfloat16)[:, None, None]
    back_state = jnp.einsum(
        "thd,the->hde", queries * mask_head, grad_out, preferred_element_type=jnp.float32
    )
    suffix, next_slab_low = backward_suffix(back_state, lows)
    place = lax.axis_index("slab")
    group = lows.shape[0]
    in_slab_next = jnp.sum(jnp.where(jnp.arange(group) == place + 1, lows, 0))
    next_low = jnp.where(place + 1 < group, in_slab_next, next_slab_low)
    continues = (next_low <= block) & (block + 1 < block_count)
    suffix = suffix * continues.astype(jnp.float32)
    suffix_low = suffix.astype(jnp.bfloat16)
    mask_tail = mask_last.astype(jnp.float32)
    grad_key = jnp.einsum("hts,thd->shd", back_weights, queries, preferred_element_type=jnp.float32)
    grad_key = grad_key + mask_tail * jnp.einsum(
        "she,hde->shd", value_vecs, suffix_low, preferred_element_type=jnp.float32
    )
    grad_value = jnp.einsum("hts,the->she", weights, grad_out, preferred_element_type=jnp.float32)
    grad_value = grad_value + mask_tail * jnp.einsum(
        "shd,hde->she", key_vecs, suffix_low, preferred_element_type=jnp.float32
    )
    flat = (tokens_here, heads_here * DH)
    return (
        normed.reshape(flat),
        grad_query.astype(jnp.bfloat16).reshape(flat),
        grad_key.astype(jnp.bfloat16).reshape(flat),
        grad_value.astype(jnp.bfloat16).reshape(flat),
    )


def solution(mesh):
    seq_count = mesh.shape["seq"]
    group = SLAB if seq_count % SLAB == 0 else 1
    slabbed = Mesh(
        mesh.devices.reshape(seq_count // group, group, mesh.shape["head"]), ("zs", "slab", "head")
    )
    rows = P(SEQ, "head")
    placed = (rows, rows, rows, rows, P("head"), P(SEQ))
    return jax.shard_map(
        on_device,
        mesh=slabbed,
        in_specs=placed,
        out_specs=(rows, rows, rows, rows),
        check_vma=False,
    )
```
